256 devices in a mesh: own: 32 (over x, z), row: 8 (over y, core).
Axes of the slice: x: 4, y: 4, z: 8, core: 2. Of those that a mesh axis runs over, the one named last changes fastest.
Arguments:
- sigma_anc: float32 [16384, 16384], P('row', 'own'), may hold values from -1.5 to 1.5
- row_blocks: int32 [64, 8], replicated, may hold values from 0 to 63, as said below
- panel1: float32 [64, 2048, 256], P('own', 'row'), may hold values from -0.375 to 0.375
- diag_inv1: float32 [64, 256, 256], P('own'), as said below
- mask1: int32 [64, 8], P('own', 'row'), may hold values 0 or 1
- parent_block2: float32 [64, 256, 256], P('own'), may hold values from -0.375 to 0.375
- panel2: float32 [64, 2048, 256], P('own', 'row'), may hold values from -0.375 to 0.375
- diag_inv2: float32 [64, 256, 256], P('own'), as said below
- mask2: int32 [64, 8], P('own', 'row'), may hold values 0 or 1
Outputs:
- sel1_panel: float32 [64, 2048, 256], P('own', 'row')
- sel1_diag: float32 [64, 256, 256], P('own')
- sel2_parent: float32 [64, 256, 256], P('own')
- sel2_panel: float32 [64, 2048, 256], P('own', 'row')
- sel2_diag: float32 [64, 256, 256], P('own')
The draws below stay inside these ranges and needn't reach their ends.
Inputs may be any that keep to these rules, and one draw needn't show every extreme that they name: `row_blocks`: entry l of each row lies in block rows 8 * l to 8 * (l + 1) - 1; for supernodes s with the same s // 2, the entries of one column l lie in different aligned runs of 2 block rows. `diag_inv1`: lower triangular, with diagonal entries from 1 to 2. `diag_inv2`: lower triangular, with diagonal entries from 1 to 2.
All inputs are finite; a program needn't handle non-finite values. No bound on the sum of `mask1` or of `mask2` on one device may be relied on, other than what follows from the above.
Results may differ from the reference program's by a relative error of at most 0.000071.
Values sent between devices are 32-bit elements; how exact they have to be, the bound alone decides.
No kernel may reach another device: no remote copies, remote signals or barrier semaphores. Data moves between devices by JAX's collectives and lax.ppermute only.
A program may use at most 128 MiB of HBM per device.

```python
import jax
import jax.numpy as jnp
from jax import lax

B = 256
AROW = 8
NSD = 2
A = 64
NS = 64
N_OWN = 32
N_ROW = 8


def lower_inverse(key):
    key_off, key_diag = jax.random.split(key)
    off = jax.random.normal(key_off, (NS, B, B), jnp.float32) * (0.8 / B ** 0.5)
    diag = jax.random.uniform(key_diag, (NS, B), jnp.float32, 1.0, 2.0)
    lower = jnp.tril(jnp.ones((B, B), jnp.float32), -1)
    return off * lower[None] + jnp.eye(B, dtype=jnp.float32)[None] * diag[:, None, :]


def draw_diag_inv1(key, part):
    return lower_inverse(jax.random.fold_in(key, 11))


def draw_diag_inv2(key, part):
    return lower_inverse(jax.random.fold_in(key, 22))


def draw_row_blocks(key, part):
    quarters = N_OWN // N_ROW
    width = AROW // quarters
    key_score, key_within = jax.random.split(jax.random.fold_in(key, 33))
    scores = jax.random.randint(key_score, (N_OWN, N_ROW, quarters), 0, 1 << 20)
    keyed = scores * quarters + jnp.arange(quarters, dtype=jnp.int32)[None, None, :]
    order = jnp.argsort(keyed, axis=-1, stable=True).astype(jnp.int32)[:, :, :NSD]
    quarter = jnp.transpose(order, (0, 2, 1)).reshape(NS, N_ROW)
    within = jax.random.randint(key_within, (NS, N_ROW), 0, width)
    base = jnp.arange(N_ROW, dtype=jnp.int32)[None, :] * AROW
    return (base + quarter * width + within).astype(jnp.int32)


def plant(entries, own_key, low, largest):
    place = [jax.random.randint(jax.random.fold_in(own_key, axis), (), 0, length) for axis, length in enumerate(entries.shape)]
    longest = entries.shape.index(max(entries.shape))
    beside = place[:longest] + [(place[longest] + 1) % entries.shape[longest]] + place[longest + 1:]
    return entries.at[tuple(place)].set(low).at[tuple(beside)].set(largest)


def level_of(key, extent, shards, least, largest):
    def one(dim, shards_of):
        draws = jax.random.uniform(jax.random.fold_in(jax.random.fold_in(key, 6), dim), (shards_of,), jnp.float32, least / len(shards), largest / len(shards))
        return jnp.repeat(jnp.exp(draws), extent[dim] // shards_of).reshape((-1,) + (1,) * (len(extent) - dim - 1))

    loudness = one(*shards[0])
    for cut in shards[1:]:
        loudness = loudness * one(*cut)
    return loudness


def gaussian(own_key, extent, scale, most, shards=(), held_as=jnp.bfloat16):
    result = scale * jax.random.normal(own_key, extent, jnp.float32)
    if shards:
        result = result * level_of(own_key, extent, shards, -0.22, 0.18)
    return jnp.clip(result, -most, most).astype(held_as)


def setup_inputs(seed: int = 0) -> dict:
    keys = jax.random.split(jax.random.key(seed), 10)
    return {
        "sigma_anc": gaussian(keys[0], (A * B, A * B), 0.1, 1.5, ((0, 8), (1, 32)), jnp.float32),
        "row_blocks": draw_row_blocks(jax.random.fold_in(keys[9], 71), 0),
        "panel1": gaussian(keys[2], (NS, N_ROW * B, B), B ** -0.5, 0.375, ((0, 32), (1, 8)), jnp.float32),
        "diag_inv1": draw_diag_inv1(jax.random.fold_in(keys[9], 71), 0),
        "mask1": plant((jax.random.randint(keys[4], (NS, N_ROW), 0, 4) < 3).astype(jnp.int32), jax.random.fold_in(keys[4], 1), 0, 1),
        "parent_block2": gaussian(keys[5], (NS, B, B), B ** -0.5, 0.375, ((0, 32),), jnp.float32),
        "panel2": gaussian(keys[6], (NS, N_ROW * B, B), B ** -0.5, 0.375, ((0, 32), (1, 8)), jnp.float32),
        "diag_inv2": draw_diag_inv2(jax.random.fold_in(keys[9], 71), 0),
        "mask2": plant((jax.random.randint(keys[8], (NS, N_ROW), 0, 4) < 3).astype(jnp.int32), jax.random.fold_in(keys[8], 1), 0, 1),
    }


HIGH = lax.Precision.HIGHEST


def product(form, left, right):
    return jnp.einsum(form, left, right, precision=HIGH)


def reference(sigma_anc, row_blocks, panel1, diag_inv1, mask1, parent_block2, panel2, diag_inv2, mask2):
    blocks4 = sigma_anc.reshape(A, B, A, B)
    keep1 = mask1.astype(jnp.float32)

    def level_one(items):
        rowlist, panel, inverse, keep = items
        picked = blocks4[rowlist[:, None], :, rowlist[None, :], :]
        factor = keep[:, None, None] * product("lij,jc->lic", panel, inverse)
        below = -keep[:, None, None] * product("lmij,mjc->lic", picked, factor)
        diagonal = product("ji,jc->ic", inverse, inverse) - product("lji,ljc->ic", factor, below)
        return below, diagonal

    sel1_blocks, sel1_diag = lax.map(level_one, (row_blocks, panel1.reshape(NS, N_ROW, B, B), diag_inv1, keep1))
    parent = (jnp.arange(NS) - NSD) % NS
    keep2 = mask2.astype(jnp.float32) * keep1[parent]

    def level_two(items):
        rowlist, par_below, par_diag, top, panel, inverse, keep = items
        picked = blocks4[rowlist[:, None], :, rowlist[None, :], :]
        up_parent = product("ij,jc->ic", top, inverse)
        factor = keep[:, None, None] * product("lij,jc->lic", panel, inverse)
        upper = -(product("ij,jc->ic", par_diag, up_parent) + product("lji,ljc->ic", par_below, factor))
        below = -keep[:, None, None] * (product("lij,jc->lic", par_below, up_parent) + product("lmij,mjc->lic", picked, factor))
        diagonal = product("ji,jc->ic", inverse, inverse) - product("ji,jc->ic", up_parent, upper) - product("lji,ljc->ic", factor, below)
        return upper, below, diagonal

    sel2_parent, sel2_blocks, sel2_diag = lax.map(level_two, (row_blocks[parent], sel1_blocks[parent], sel1_diag[parent], parent_block2, panel2.reshape(NS, N_ROW, B, B), diag_inv2, keep2))
    return (sel1_blocks.reshape(NS, N_ROW * B, B), sel1_diag, sel2_parent, sel2_blocks.reshape(NS, N_ROW * B, B), sel2_diag)
```

```python
import jax
import jax.numpy as jnp
from jax import lax
from jax.sharding import PartitionSpec as P

B = 256


HIGH = lax.Precision.HIGHEST


def shifted(shard, axis, by):
    length = lax.axis_size(axis)
    return lax.ppermute(shard, axis, [(i, (i + by) % length) for i in range(length)])


def product(form, left, right):
    return jnp.einsum(form, left, right, precision=HIGH)


def select_send(sigma_local, row_blocks, slots):
    own_count = lax.axis_size("own")
    own_here = lax.axis_index("own")
    row_here = lax.axis_index("row")
    rows_here = sigma_local.shape[0] // B
    cols_here = sigma_local.shape[1] // B
    rowlist = row_blocks.reshape(own_count, slots, -1)
    group = own_here * cols_here // rows_here
    want_col = lax.dynamic_index_in_dim(rowlist, group, 2, keepdims=False)
    local_col = want_col - own_here * cols_here
    match = ((local_col >= 0) & (local_col < cols_here)).astype(jnp.int32)
    which = jnp.sum(match * jnp.arange(slots, dtype=jnp.int32)[None, :], axis=1)
    chosen = rowlist[jnp.arange(own_count, dtype=jnp.int32), which]
    chosen_row = (
        lax.dynamic_index_in_dim(chosen, row_here, 1, keepdims=False) - row_here * rows_here
    )
    chosen_col = jnp.clip(
        lax.dynamic_index_in_dim(chosen, group, 1, keepdims=False) - own_here * cols_here,
        0,
        cols_here - 1,
    )
    blocks4 = sigma_local.reshape(rows_here, B, cols_here, B)
    return blocks4[chosen_row, :, chosen_col, :]


def select_take(received, row_blocks, slots, cols_here):
    mine = lax.axis_index("own") * slots + jnp.arange(slots, dtype=jnp.int32)
    rowlist = row_blocks[mine]
    sender = rowlist // cols_here
    return received[sender]


def on_device(
    sigma_anc, row_blocks, panel1, diag_inv1, mask1, parent_block2, panel2, diag_inv2, mask2
):
    slots = panel1.shape[0]
    cols_here = sigma_anc.shape[1] // B
    keep_own2 = mask2.astype(jnp.float32)
    up_parent = product("kij,kjc->kic", parent_block2, diag_inv2)
    factor2_own = keep_own2[:, :, None] * product("kij,kjc->kic", panel2, diag_inv2)
    factor2_child = shifted(factor2_own, "own", -1)

    outgoing = select_send(sigma_anc, row_blocks, slots)
    received = lax.all_to_all(outgoing, "own", split_axis=0, concat_axis=0, tiled=True)
    blocks1 = select_take(received, row_blocks, slots, cols_here)
    keep1 = mask1.astype(jnp.float32)
    factor1 = keep1[:, :, None] * product("kij,kjc->kic", panel1, diag_inv1)
    factors1 = lax.all_gather(factor1, "row", axis=1, tiled=True).reshape(slots, -1, B, B)
    sel1_panel = -keep1[:, :, None] * product("kmij,kmjc->kic", blocks1, factors1)
    gram1 = product("kji,kjc->kic", diag_inv1, diag_inv1)
    sel1_diag = gram1 - lax.psum(product("kji,kjc->kic", factor1, sel1_panel), "row")

    factor2 = keep1[:, :, None] * factor2_child
    factors2 = lax.all_gather(factor2, "row", axis=1, tiled=True).reshape(slots, -1, B, B)
    anc2 = keep1[:, :, None] * product("kmij,kmjc->kic", blocks1, factors2)

    par_panel = shifted(sel1_panel, "own", 1)
    par_anc = shifted(anc2, "own", 1)
    par_diag = shifted(sel1_diag, "own", 1)

    sel2_panel = -keep_own2[:, :, None] * (
        product("kij,kjc->kic", par_panel, up_parent) + par_anc
    )
    cross = product("kji,kjc->kic", par_panel, factor2_own)
    back = product("kji,kjc->kic", factor2_own, sel2_panel)
    par_diag, cross, back = lax.optimization_barrier((par_diag, cross, back))
    cross, back = lax.psum((cross, back), "row")
    sel2_parent = -(product("kij,kjc->kic", par_diag, up_parent) + cross)
    gram2 = product("kji,kjc->kic", diag_inv2, diag_inv2)
    sel2_diag = gram2 - product("kji,kjc->kic", up_parent, sel2_parent) - back
    return (sel1_panel, sel1_diag, sel2_parent, sel2_panel, sel2_diag)


def solution(mesh):
    in_specs = (
        P("row", "own"),
        P(),
        P("own", "row", None),
        P("own", None, None),
        P("own", "row"),
        P("own", None, None),
        P("own", "row", None),
        P("own", None, None),
        P("own", "row"),
    )
    out_specs = (
        P("own", "row", None),
        P("own", None, None),
        P("own", None, None),
        P("own", "row", None),
        P("own", None, None),
    )
    return jax.shard_map(
        on_device, mesh=mesh, in_specs=in_specs, out_specs=out_specs, check_vma=False
    )
```

```python
import jax
import jax.numpy as jnp
from jax import lax
from jax.experimental import pallas as pl
from jax.experimental.pallas import tpu as pltpu
from jax.sharding import PartitionSpec as P

B = 256


HIGH = lax.Precision.HIGHEST


def shifted(shard, axis, by):
    length = lax.axis_size(axis)
    return lax.ppermute(shard, axis, [(i, (i + by) % length) for i in range(length)])


def row_sum(x):
    length = lax.axis_size("row")
    step = 1
    while step < length:
        x = x + lax.ppermute(x, "row", [(i, i ^ step) for i in range(length)])
        step *= 2
    return x


def product(form, left, right):
    return jnp.einsum(form, left, right, precision=HIGH)


def _copy_block(rows_ref, cols_ref, src_ref, out_ref):
    out_ref[0] = src_ref[...]


def gather_blocks(src, rows, cols):
    count = rows.shape[0]
    grid_spec = pltpu.PrefetchScalarGridSpec(
        num_scalar_prefetch=2,
        grid=(count,),
        in_specs=[pl.BlockSpec((B, B), lambda i, r, c: (r[i], c[i]))],
        out_specs=pl.BlockSpec((1, B, B), lambda i, r, c: (i, 0, 0)),
    )
    return pl.pallas_call(
        _copy_block,
        out_shape=jax.ShapeDtypeStruct((count, B, B), src.dtype),
        grid_spec=grid_spec,
        cost_estimate=pl.CostEstimate(
            flops=0, bytes_accessed=2 * count * B * B * 4, transcendentals=0
        ),
    )(rows, cols, src)


def select_send(sigma_local, row_blocks, slots):
    own_count = lax.axis_size("own")
    own_here = lax.axis_index("own")
    row_here = lax.axis_index("row")
    rows_here = sigma_local.shape[0] // B
    cols_here = sigma_local.shape[1] // B
    rowlist = row_blocks.reshape(own_count, slots, -1)
    group = own_here * cols_here // rows_here
    want_col = lax.dynamic_index_in_dim(rowlist, group, 2, keepdims=False)
    local_col = want_col - own_here * cols_here
    match = ((local_col >= 0) & (local_col < cols_here)).astype(jnp.int32)
    which = jnp.sum(match * jnp.arange(slots, dtype=jnp.int32)[None, :], axis=1)
    chosen = rowlist[jnp.arange(own_count, dtype=jnp.int32), which]
    chosen_row = jnp.clip(
        lax.dynamic_index_in_dim(chosen, row_here, 1, keepdims=False) - row_here * rows_here,
        0,
        rows_here - 1,
    )
    chosen_col = jnp.clip(
        lax.dynamic_index_in_dim(chosen, group, 1, keepdims=False) - own_here * cols_here,
        0,
        cols_here - 1,
    )
    return gather_blocks(sigma_local, chosen_row, chosen_col)


def select_take(received, row_blocks, slots, cols_here):
    mine = lax.axis_index("own") * slots + jnp.arange(slots, dtype=jnp.int32)
    rowlist = row_blocks[mine]
    sender = rowlist // cols_here
    return received[sender]


def on_device(
    sigma_anc, row_blocks, panel1, diag_inv1, mask1, parent_block2, panel2, diag_inv2, mask2
):
    slots = panel1.shape[0]
    cols_here = sigma_anc.shape[1] // B
    keep_own2 = mask2.astype(jnp.float32)
    factor2_own = keep_own2[:, :, None] * product("kij,kjc->kic", panel2, diag_inv2)
    factor2_child = shifted(factor2_own, "own", -1)

    outgoing = select_send(sigma_anc, row_blocks, slots)
    factor2_child, outgoing = lax.optimization_barrier((factor2_child, outgoing))
    received = lax.all_to_all(outgoing, "own", split_axis=0, concat_axis=0, tiled=True)

    keep1 = mask1.astype(jnp.float32)
    factor1 = keep1[:, :, None] * product("kij,kjc->kic", panel1, diag_inv1)
    factor2 = keep1[:, :, None] * factor2_child
    both = jnp.concatenate([factor1, factor2], axis=-1)
    boths = lax.all_gather(both, "row", axis=1, tiled=True).reshape(slots, -1, B, 2 * B)

    blocks1 = select_take(received, row_blocks, slots, cols_here)
    kept = keep1[:, :, None] * product("kmij,kmjc->kic", blocks1, boths)
    sel1_panel = -kept[:, :, :B]
    gram1 = product("kji,kjc->kic", diag_inv1, diag_inv1)
    sel1_diag = gram1 - row_sum(product("kji,kjc->kic", factor1, sel1_panel))

    par_kept = shifted(kept, "own", 1)
    par_diag = shifted(sel1_diag, "own", 1)
    par_panel = -par_kept[:, :, :B]
    par_anc = par_kept[:, :, B:]

    up_parent = product("kij,kjc->kic", parent_block2, diag_inv2)
    sel2_panel = -keep_own2[:, :, None] * (
        product("kij,kjc->kic", par_panel, up_parent) + par_anc
    )
    cross = product("kji,kjc->kic", par_panel, factor2_own)
    back = product("kji,kjc->kic", factor2_own, sel2_panel)
    summed = row_sum(jnp.concatenate([cross, back], axis=-1))
    cross = summed[:, :, :B]
    back = summed[:, :, B:]
    sel2_parent = -(product("kij,kjc->kic", par_diag, up_parent) + cross)
    gram2 = product("kji,kjc->kic", diag_inv2, diag_inv2)
    sel2_diag = gram2 - product("kji,kjc->kic", up_parent, sel2_parent) - back
    return (sel1_panel, sel1_diag, sel2_parent, sel2_panel, sel2_diag)


def solution(mesh):
    in_specs = (
        P("row", "own"),
        P(),
        P("own", "row", None),
        P("own", None, None),
        P("own", "row"),
        P("own", None, None),
        P("own", "row", None),
        P("own", None, None),
        P("own", "row"),
    )
    out_specs = (
        P("own", "row", None),
        P("own", None, None),
        P("own", None, None),
        P("own", "row", None),
        P("own", None, None),
    )
    return jax.shard_map(
        on_device, mesh=mesh, in_specs=in_specs, out_specs=out_specs, check_vma=False
    )
```

```python
import jax
import jax.numpy as jnp
from jax import lax
from jax.experimental import pallas as pl
from jax.experimental.pallas import tpu as pltpu
from jax.sharding import PartitionSpec as P

B = 256


HIGH = lax.Precision.HIGHEST


def shifted(shard, axis, by):
    length = lax.axis_size(axis)
    return lax.ppermute(shard, axis, [(i, (i + by) % length) for i in range(length)])


def row_sum(x):
    length = lax.axis_size("row")
    core = lax.axis_index("row") % 2
    half = x.shape[1] // 2
    lo, hi = x[:, :half], x[:, half:]
    mine = jnp.where(core == 0, lo, hi)
    other = jnp.where(core == 0, hi, lo)
    partner = [(i, i ^ 1) for i in range(length)]
    part = mine + lax.ppermute(other, "row", partner)
    step = 2
    while step < length:
        part = part + lax.ppermute(part, "row", [(i, i ^ step) for i in range(length)])
        step *= 2
    got = lax.ppermute(part, "row", partner)
    return jnp.where(
        core == 0, jnp.concatenate([part, got], axis=1), jnp.concatenate([got, part], axis=1)
    )


def product(form, left, right):
    return jnp.einsum(form, left, right, precision=HIGH)


def _copy_blocks(rows_ref, cols_ref, src_ref, out_ref, staged, sem_in, sems_out):
    load = pltpu.make_async_copy(src_ref, staged, sem_in)
    load.start()
    load.wait()
    count = out_ref.shape[0]
    copies = []
    for i in range(count):
        copy = pltpu.make_async_copy(
            staged.at[pl.ds(rows_ref[i] * B, B), pl.ds(pl.multiple_of(cols_ref[i] * B, B), B)],
            out_ref.at[i],
            sems_out.at[i],
        )
        copy.start()
        copies.append(copy)
    for copy in copies:
        copy.wait()


def gather_blocks(src, rows, cols):
    count = rows.shape[0]
    grid_spec = pltpu.PrefetchScalarGridSpec(
        num_scalar_prefetch=2,
        grid=(),
        in_specs=[pl.BlockSpec(memory_space=pl.ANY)],
        out_specs=pl.BlockSpec(memory_space=pl.ANY),
        scratch_shapes=[
            pltpu.VMEM(src.shape, src.dtype),
            pltpu.SemaphoreType.DMA(()),
            pltpu.SemaphoreType.DMA((count,)),
        ],
    )
    return pl.pallas_call(
        _copy_blocks,
        out_shape=jax.ShapeDtypeStruct((count, B, B), src.dtype),
        grid_spec=grid_spec,
        cost_estimate=pl.CostEstimate(
            flops=0, bytes_accessed=(src.size + count * B * B) * 4, transcendentals=0
        ),
    )(rows, cols, src)


def select_send(sigma_local, row_blocks, slots):
    own_count = lax.axis_size("own")
    own_here = lax.axis_index("own")
    row_here = lax.axis_index("row")
    rows_here = sigma_local.shape[0] // B
    cols_here = sigma_local.shape[1] // B
    rowlist = row_blocks.reshape(own_count, slots, -1)
    group = own_here * cols_here // rows_here
    want_col = lax.dynamic_index_in_dim(rowlist, group, 2, keepdims=False)
    local_col = want_col - own_here * cols_here
    match = ((local_col >= 0) & (local_col < cols_here)).astype(jnp.int32)
    which = jnp.sum(match * jnp.arange(slots, dtype=jnp.int32)[None, :], axis=1)
    chosen = rowlist[jnp.arange(own_count, dtype=jnp.int32), which]
    chosen_row = jnp.clip(
        lax.dynamic_index_in_dim(chosen, row_here, 1, keepdims=False) - row_here * rows_here,
        0,
        rows_here - 1,
    )
    chosen_col = jnp.clip(
        lax.dynamic_index_in_dim(chosen, group, 1, keepdims=False) - own_here * cols_here,
        0,
        cols_here - 1,
    )
    return gather_blocks(sigma_local, chosen_row, chosen_col)


def select_take(received, row_blocks, slots, cols_here):
    mine = lax.axis_index("own") * slots + jnp.arange(slots, dtype=jnp.int32)
    rowlist = row_blocks[mine]
    sender = rowlist // cols_here
    return received[sender]


def on_device(
    sigma_anc, row_blocks, panel1, diag_inv1, mask1, parent_block2, panel2, diag_inv2, mask2
):
    slots = panel1.shape[0]
    cols_here = sigma_anc.shape[1] // B
    keep_own2 = mask2.astype(jnp.float32)
    factor2_own = keep_own2[:, :, None] * product("kij,kjc->kic", panel2, diag_inv2)
    factor2_child = shifted(factor2_own, "own", -1)

    outgoing = select_send(sigma_anc, row_blocks, slots)
    factor2_child, outgoing = lax.optimization_barrier((factor2_child, outgoing))
    received = lax.all_to_all(outgoing, "own", split_axis=0, concat_axis=0, tiled=True)

    keep1 = mask1.astype(jnp.float32)
    factor1 = keep1[:, :, None] * product("kij,kjc->kic", panel1, diag_inv1)
    factor2 = keep1[:, :, None] * factor2_child
    both = jnp.concatenate([factor1, factor2], axis=-1)
    boths = lax.all_gather(both, "row", axis=1, tiled=True).reshape(slots, -1, B, 2 * B)

    blocks1 = select_take(received, row_blocks, slots, cols_here)
    kept = keep1[:, :, None] * product("kmij,kmjc->kic", blocks1, boths)
    sel1_panel = -kept[:, :, :B]
    gram1 = product("kji,kjc->kic", diag_inv1, diag_inv1)
    sel1_diag = gram1 - row_sum(product("kji,kjc->kic", factor1, sel1_panel))

    par_kept = shifted(kept, "own", 1)
    par_diag = shifted(sel1_diag, "own", 1)
    par_panel = -par_kept[:, :, :B]
    par_anc = par_kept[:, :, B:]

    up_parent = product("kij,kjc->kic", parent_block2, diag_inv2)
    sel2_panel = -keep_own2[:, :, None] * (
        product("kij,kjc->kic", par_panel, up_parent) + par_anc
    )
    cross = product("kji,kjc->kic", par_panel, factor2_own)
    back = product("kji,kjc->kic", factor2_own, sel2_panel)
    summed = row_sum(jnp.concatenate([cross, back], axis=-1))
    cross = summed[:, :, :B]
    back = summed[:, :, B:]
    sel2_parent = -(product("kij,kjc->kic", par_diag, up_parent) + cross)
    gram2 = product("kji,kjc->kic", diag_inv2, diag_inv2)
    sel2_diag = gram2 - product("kji,kjc->kic", up_parent, sel2_parent) - back
    return (sel1_panel, sel1_diag, sel2_parent, sel2_panel, sel2_diag)


def solution(mesh):
    in_specs = (
        P("row", "own"),
        P(),
        P("own", "row", None),
        P("own", None, None),
        P("own", "row"),
        P("own", None, None),
        P("own", "row", None),
        P("own", None, None),
        P("own", "row"),
    )
    out_specs = (
        P("own", "row", None),
        P("own", None, None),
        P("own", None, None),
        P("own", "row", None),
        P("own", None, None),
    )
    return jax.shard_map(
        on_device, mesh=mesh, in_specs=in_specs, out_specs=out_specs, check_vma=False
    )
```

```python
import jax
import jax.numpy as jnp
from jax import lax
from jax.experimental import pallas as pl
from jax.experimental.pallas import tpu as pltpu
from jax.sharding import PartitionSpec as P

B = 256


HIGH = lax.Precision.HIGHEST


def shifted(shard, axis, by):
    length = lax.axis_size(axis)
    return lax.ppermute(shard, axis, [(i, (i + by) % length) for i in range(length)])


def row_sum(x):
    length = lax.axis_size("row")
    core = lax.axis_index("row") % 2
    half = x.shape[1] // 2
    lo, hi = x[:, :half], x[:, half:]
    mine = jnp.where(core == 0, lo, hi)
    other = jnp.where(core == 0, hi, lo)
    partner = [(i, i ^ 1) for i in range(length)]
    part = mine + lax.ppermute(other, "row", partner)
    step = 2
    while step < length:
        part = part + lax.ppermute(part, "row", [(i, i ^ step) for i in range(length)])
        step *= 2
    got = lax.ppermute(part, "row", partner)
    return jnp.where(
        core == 0, jnp.concatenate([part, got], axis=1), jnp.concatenate([got, part], axis=1)
    )


def product(form, left, right):
    return jnp.einsum(form, left, right, precision=HIGH)


def _copy_blocks(rows_ref, cols_ref, src_ref, out_ref, staged, sem_in, sems_out):
    load = pltpu.make_async_copy(src_ref, staged, sem_in)
    load.start()
    load.wait()
    count = out_ref.shape[0]
    copies = []
    for i in range(count):
        copy = pltpu.make_async_copy(
            staged.at[pl.ds(rows_ref[i] * B, B), pl.ds(pl.multiple_of(cols_ref[i] * B, B), B)],
            out_ref.at[i],
            sems_out.at[i],
        )
        copy.start()
        copies.append(copy)
    for copy in copies:
        copy.wait()


def gather_blocks(src, rows, cols):
    count = rows.shape[0]
    grid_spec = pltpu.PrefetchScalarGridSpec(
        num_scalar_prefetch=2,
        grid=(),
        in_specs=[pl.BlockSpec(memory_space=pl.ANY)],
        out_specs=pl.BlockSpec(memory_space=pl.ANY),
        scratch_shapes=[
            pltpu.VMEM(src.shape, src.dtype),
            pltpu.SemaphoreType.DMA(()),
            pltpu.SemaphoreType.DMA((count,)),
        ],
    )
    return pl.pallas_call(
        _copy_blocks,
        out_shape=jax.ShapeDtypeStruct((count, B, B), src.dtype),
        grid_spec=grid_spec,
        cost_estimate=pl.CostEstimate(
            flops=0, bytes_accessed=(src.size + count * B * B) * 4, transcendentals=0
        ),
    )(rows, cols, src)


def select_send(sigma_local, row_blocks, slots):
    own_count = lax.axis_size("own")
    own_here = lax.axis_index("own")
    row_here = lax.axis_index("row")
    rows_here = sigma_local.shape[0] // B
    cols_here = sigma_local.shape[1] // B
    rowlist = row_blocks.reshape(own_count, slots, -1)
    group = own_here * cols_here // rows_here
    want_col = lax.dynamic_index_in_dim(rowlist, group, 2, keepdims=False)
    local_col = want_col - own_here * cols_here
    match = ((local_col >= 0) & (local_col < cols_here)).astype(jnp.int32)
    which = jnp.sum(match * jnp.arange(slots, dtype=jnp.int32)[None, :], axis=1)
    chosen = rowlist[jnp.arange(own_count, dtype=jnp.int32), which]
    chosen_row = jnp.clip(
        lax.dynamic_index_in_dim(chosen, row_here, 1, keepdims=False) - row_here * rows_here,
        0,
        rows_here - 1,
    )
    chosen_col = jnp.clip(
        lax.dynamic_index_in_dim(chosen, group, 1, keepdims=False) - own_here * cols_here,
        0,
        cols_here - 1,
    )
    return gather_blocks(sigma_local, chosen_row, chosen_col)


def select_take(received, row_blocks, slots, cols_here):
    mine = lax.axis_index("own") * slots + jnp.arange(slots, dtype=jnp.int32)
    rowlist = row_blocks[mine]
    sender = rowlist // cols_here
    return received[sender]


def on_device(
    sigma_anc, row_blocks, panel1, diag_inv1, mask1, parent_block2, panel2, diag_inv2, mask2
):
    slots = panel1.shape[0]
    cols_here = sigma_anc.shape[1] // B
    row_count = lax.axis_size("row")
    row_here = lax.axis_index("row")
    core = row_here % 2
    keep_own2 = mask2.astype(jnp.float32)
    factor2_own = keep_own2[:, :, None] * product("kij,kjc->kic", panel2, diag_inv2)
    piece = B // row_count
    up_own = lax.dynamic_slice_in_dim(parent_block2, row_here * piece, piece, axis=1)
    up_own = product("kij,kjc->kic", up_own, diag_inv2)
    payload = shifted(jnp.concatenate([factor2_own, up_own], axis=1), "own", -1)

    outgoing = select_send(sigma_anc, row_blocks, slots)
    payload, outgoing = lax.optimization_barrier((payload, outgoing))
    received = lax.all_to_all(outgoing, "own", split_axis=0, concat_axis=0, tiled=True)

    keep1 = mask1.astype(jnp.float32)
    factor1 = keep1[:, :, None] * product("kij,kjc->kic", panel1, diag_inv1)
    factor2 = keep1[:, :, None] * payload[:, :B]
    both = jnp.concatenate([factor1, factor2], axis=-1)
    boths = lax.all_gather(both, "row", axis=1, tiled=True).reshape(slots, -1, B, 2 * B)
    up_parent = lax.all_gather(payload[:, B:], "row", axis=1, tiled=True)

    blocks1 = select_take(received, row_blocks, slots, cols_here)
    kept = keep1[:, :, None] * product("kmij,kmjc->kic", blocks1, boths)
    sel1_panel = -kept[:, :, :B]
    pre2 = -(product("kij,kjc->kic", sel1_panel, up_parent) + kept[:, :, B:])
    pre2_child = shifted(pre2, "own", 1)
    terms = jnp.concatenate(
        [
            product("kji,kjc->kic", factor1, sel1_panel),
            product("kji,kjc->kic", sel1_panel, factor2),
            product("kji,kjc->kic", factor2, pre2),
        ],
        axis=-1,
    )
    summed = row_sum(terms)
    gram1 = product("kji,kjc->kic", diag_inv1, diag_inv1)
    sel1_diag = gram1 - summed[:, :, :B]
    sel2_parent = -(product("kij,kjc->kic", sel1_diag, up_parent) + summed[:, :, B : 2 * B])
    down = product("kji,kjc->kic", up_parent, sel2_parent) + summed[:, :, 2 * B :]

    partner = [(i, i ^ 1) for i in range(row_count)]
    got = shifted(jnp.where(core == 0, sel2_parent, down), "own", 1)
    other = lax.ppermute(got, "row", partner)
    sel2_parent_child = jnp.where(core == 0, got, other)
    down_child = jnp.where(core == 0, other, got)

    sel2_panel = keep_own2[:, :, None] * pre2_child
    gram2 = product("kji,kjc->kic", diag_inv2, diag_inv2)
    sel2_diag = gram2 - down_child
    return (sel1_panel, sel1_diag, sel2_parent_child, sel2_panel, sel2_diag)


def solution(mesh):
    in_specs = (
        P("row", "own"),
        P(),
        P("own", "row", None),
        P("own", None, None),
        P("own", "row"),
        P("own", None, None),
        P("own", "row", None),
        P("own", None, None),
        P("own", "row"),
    )
    out_specs = (
        P("own", "row", None),
        P("own", None, None),
        P("own", None, None),
        P("own", "row", None),
        P("own", None, None),
    )
    return jax.shard_map(
        on_device, mesh=mesh, in_specs=in_specs, out_specs=out_specs, check_vma=False
    )
```

```python
import jax
import jax.numpy as jnp
from jax import lax
from jax.experimental import pallas as pl
from jax.experimental.pallas import tpu as pltpu
from jax.sharding import PartitionSpec as P

B = 256


HIGH = lax.Precision.HIGHEST


def shifted(shard, axis, by):
    length = lax.axis_size(axis)
    return lax.ppermute(shard, axis, [(i, (i + by) % length) for i in range(length)])


def row_sum(x, arrive=None):
    length = lax.axis_size("row")
    core = lax.axis_index("row") % 2
    half = x.shape[1] // 2
    lo, hi = x[:, :half], x[:, half:]
    mine = jnp.where(core == 0, lo, hi)
    other = jnp.where(core == 0, hi, lo)
    partner = [(i, i ^ 1) for i in range(length)]
    part = mine + lax.ppermute(other, "row", partner)
    step = 2
    while step < length:
        part = part + lax.ppermute(part, "row", [(i, i ^ step) for i in range(length)])
        step *= 2
    if arrive is not None:
        arrive, part = lax.optimization_barrier((arrive, part))
    got = lax.ppermute(part, "row", partner)
    full = jnp.where(
        core == 0, jnp.concatenate([part, got], axis=1), jnp.concatenate([got, part], axis=1)
    )
    return full, arrive


def product(form, left, right):
    return jnp.einsum(form, left, right, precision=HIGH)


def _copy_blocks(rows_ref, cols_ref, src_ref, out_ref, staged, sem_in, sems_out):
    load = pltpu.make_async_copy(src_ref, staged, sem_in)
    load.start()
    load.wait()
    count = out_ref.shape[0]
    copies = []
    for i in range(count):
        copy = pltpu.make_async_copy(
            staged.at[pl.ds(rows_ref[i] * B, B), pl.ds(pl.multiple_of(cols_ref[i] * B, B), B)],
            out_ref.at[i],
            sems_out.at[i],
        )
        copy.start()
        copies.append(copy)
    for copy in copies:
        copy.wait()


def gather_blocks(src, rows, cols):
    count = rows.shape[0]
    grid_spec = pltpu.PrefetchScalarGridSpec(
        num_scalar_prefetch=2,
        grid=(),
        in_specs=[pl.BlockSpec(memory_space=pl.ANY)],
        out_specs=pl.BlockSpec(memory_space=pl.ANY),
        scratch_shapes=[
            pltpu.VMEM(src.shape, src.dtype),
            pltpu.SemaphoreType.DMA(()),
            pltpu.SemaphoreType.DMA((count,)),
        ],
    )
    return pl.pallas_call(
        _copy_blocks,
        out_shape=jax.ShapeDtypeStruct((count, B, B), src.dtype),
        grid_spec=grid_spec,
        cost_estimate=pl.CostEstimate(
            flops=0, bytes_accessed=(src.size + count * B * B) * 4, transcendentals=0
        ),
    )(rows, cols, src)


def select_send(sigma_local, row_blocks, slots):
    own_count = lax.axis_size("own")
    own_here = lax.axis_index("own")
    row_here = lax.axis_index("row")
    rows_here = sigma_local.shape[0] // B
    cols_here = sigma_local.shape[1] // B
    rowlist = row_blocks.reshape(own_count, slots, -1)
    group = own_here * cols_here // rows_here
    want_col = lax.dynamic_index_in_dim(rowlist, group, 2, keepdims=False)
    local_col = want_col - own_here * cols_here
    match = ((local_col >= 0) & (local_col < cols_here)).astype(jnp.int32)
    which = jnp.sum(match * jnp.arange(slots, dtype=jnp.int32)[None, :], axis=1)
    chosen = rowlist[jnp.arange(own_count, dtype=jnp.int32), which]
    chosen_row = jnp.clip(
        lax.dynamic_index_in_dim(chosen, row_here, 1, keepdims=False) - row_here * rows_here,
        0,
        rows_here - 1,
    )
    chosen_col = jnp.clip(
        lax.dynamic_index_in_dim(chosen, group, 1, keepdims=False) - own_here * cols_here,
        0,
        cols_here - 1,
    )
    return gather_blocks(sigma_local, chosen_row, chosen_col)


def _take_blocks(which_ref, src_ref, out_ref, staged, sems_in, sem_out):
    count = staged.shape[0]
    copies = []
    for i in range(count):
        copy = pltpu.make_async_copy(src_ref.at[which_ref[i]], staged.at[i], sems_in.at[i])
        copy.start()
        copies.append(copy)
    for copy in copies:
        copy.wait()
    store = pltpu.make_async_copy(staged, out_ref, sem_out)
    store.start()
    store.wait()


def select_take(received, row_blocks, slots, cols_here):
    mine = lax.axis_index("own") * slots + jnp.arange(slots, dtype=jnp.int32)
    rowlist = row_blocks[mine]
    sender = jnp.clip(rowlist // cols_here, 0, received.shape[0] - 1).reshape(-1)
    count = sender.shape[0]
    grid_spec = pltpu.PrefetchScalarGridSpec(
        num_scalar_prefetch=1,
        grid=(),
        in_specs=[pl.BlockSpec(memory_space=pl.ANY)],
        out_specs=pl.BlockSpec(memory_space=pl.ANY),
        scratch_shapes=[
            pltpu.VMEM((count, B, B), received.dtype),
            pltpu.SemaphoreType.DMA((count,)),
            pltpu.SemaphoreType.DMA(()),
        ],
    )
    taken = pl.pallas_call(
        _take_blocks,
        out_shape=jax.ShapeDtypeStruct((count, B, B), received.dtype),
        grid_spec=grid_spec,
        cost_estimate=pl.CostEstimate(
            flops=0, bytes_accessed=2 * count * B * B * 4, transcendentals=0
        ),
    )(sender, received)
    return taken.reshape(slots, -1, B, B)


def on_device(
    sigma_anc, row_blocks, panel1, diag_inv1, mask1, parent_block2, panel2, diag_inv2, mask2
):
    slots = panel1.shape[0]
    cols_here = sigma_anc.shape[1] // B
    row_count = lax.axis_size("row")
    row_here = lax.axis_index("row")
    core = row_here % 2
    keep_own2 = mask2.astype(jnp.float32)
    factor2_own = keep_own2[:, :, None] * product("kij,kjc->kic", panel2, diag_inv2)
    piece = B // row_count
    up_own = lax.dynamic_slice_in_dim(parent_block2, row_here * piece, piece, axis=1)
    up_own = product("kij,kjc->kic", up_own, diag_inv2)
    payload = shifted(jnp.concatenate([factor2_own, up_own], axis=1), "own", -1)

    outgoing = select_send(sigma_anc, row_blocks, slots)
    payload, outgoing = lax.optimization_barrier((payload, outgoing))
    received = lax.all_to_all(outgoing, "own", split_axis=0, concat_axis=0, tiled=True)

    keep1 = mask1.astype(jnp.float32)
    factor1 = keep1[:, :, None] * product("kij,kjc->kic", panel1, diag_inv1)
    factor2 = keep1[:, :, None] * payload[:, :B]
    both = jnp.concatenate([factor1, factor2], axis=-1)
    boths = lax.all_gather(both, "row", axis=1, tiled=True).reshape(slots, -1, B, 2 * B)
    up_parent = lax.all_gather(payload[:, B:], "row", axis=1, tiled=True)

    blocks1 = select_take(received, row_blocks, slots, cols_here)
    kept = keep1[:, :, None] * product("kmij,kmjc->kic", blocks1, boths)
    sel1_panel = -kept[:, :, :B]
    pre2 = -(product("kij,kjc->kic", sel1_panel, up_parent) + kept[:, :, B:])
    pre2_child = shifted(pre2, "own", 1)
    terms = jnp.concatenate(
        [
            product("kji,kjc->kic", factor1, sel1_panel),
            product("kji,kjc->kic", sel1_panel, factor2),
            product("kji,kjc->kic", factor2, pre2),
        ],
        axis=-1,
    )
    summed, pre2_child = row_sum(terms, pre2_child)
    gram1 = product("kji,kjc->kic", diag_inv1, diag_inv1)
    sel1_diag = gram1 - summed[:, :, :B]
    sel2_parent = -(product("kij,kjc->kic", sel1_diag, up_parent) + summed[:, :, B : 2 * B])
    down = product("kji,kjc->kic", up_parent, sel2_parent) + summed[:, :, 2 * B :]

    partner = [(i, i ^ 1) for i in range(row_count)]
    got = shifted(jnp.where(core == 0, sel2_parent, down), "own", 1)
    other = lax.ppermute(got, "row", partner)
    sel2_parent_child = jnp.where(core == 0, got, other)
    down_child = jnp.where(core == 0, other, got)

    sel2_panel = keep_own2[:, :, None] * pre2_child
    gram2 = product("kji,kjc->kic", diag_inv2, diag_inv2)
    sel2_diag = gram2 - down_child
    return (sel1_panel, sel1_diag, sel2_parent_child, sel2_panel, sel2_diag)


def solution(mesh):
    in_specs = (
        P("row", "own"),
        P(),
        P("own", "row", None),
        P("own", None, None),
        P("own", "row"),
        P("own", None, None),
        P("own", "row", None),
        P("own", None, None),
        P("own", "row"),
    )
    out_specs = (
        P("own", "row", None),
        P("own", None, None),
        P("own", None, None),
        P("own", "row", None),
        P("own", None, None),
    )
    return jax.shard_map(
        on_device, mesh=mesh, in_specs=in_specs, out_specs=out_specs, check_vma=False
    )
```

```python
import jax
import jax.numpy as jnp
from jax import lax
from jax.experimental import pallas as pl
from jax.experimental.pallas import tpu as pltpu
from jax.sharding import PartitionSpec as P

B = 256


HIGH = lax.Precision.HIGHEST


def shifted(shard, axis, by):
    length = lax.axis_size(axis)
    return lax.ppermute(shard, axis, [(i, (i + by) % length) for i in range(length)])


def row_sum(x, arrive=None):
    length = lax.axis_size("row")
    row_here = lax.axis_index("row")
    core = row_here % 2
    chip = row_here // 2
    chips = length // 2
    half = x.shape[1] // 2
    lo, hi = x[:, :half], x[:, half:]
    mine = jnp.where(core == 0, lo, hi)
    other = jnp.where(core == 0, hi, lo)
    partner = [(i, i ^ 1) for i in range(length)]
    part = mine + lax.ppermute(other, "row", partner)
    quarter = half // chips

    def towards(value, by):
        return lax.ppermute(value, "row", [(i, (i + 2 * by) % length) for i in range(length)])

    total = lax.dynamic_slice_in_dim(part, chip * quarter, quarter, axis=1)
    for by in range(1, chips):
        target = (chip + by) % chips
        total = total + towards(lax.dynamic_slice_in_dim(part, target * quarter, quarter, axis=1), by)
    if arrive is not None:
        arrive, total = lax.optimization_barrier((arrive, total))
    pieces = [total] + [towards(total, by) for by in range(1, chips)]
    stacked = jnp.stack(pieces)
    order = (chip - jnp.arange(chips, dtype=jnp.int32)) % chips
    part = stacked[order].transpose(1, 0, 2, 3).reshape(part.shape)
    got = lax.ppermute(part, "row", partner)
    full = jnp.where(
        core == 0, jnp.concatenate([part, got], axis=1), jnp.concatenate([got, part], axis=1)
    )
    return full, arrive


def product(form, left, right):
    return jnp.einsum(form, left, right, precision=HIGH)


def _copy_blocks(rows_ref, cols_ref, src_ref, out_ref, staged, sem_in, sems_out):
    load = pltpu.make_async_copy(src_ref, staged, sem_in)
    load.start()
    load.wait()
    count = out_ref.shape[0]
    copies = []
    for i in range(count):
        copy = pltpu.make_async_copy(
            staged.at[pl.ds(rows_ref[i] * B, B), pl.ds(pl.multiple_of(cols_ref[i] * B, B), B)],
            out_ref.at[i],
            sems_out.at[i],
        )
        copy.start()
        copies.append(copy)
    for copy in copies:
        copy.wait()


def gather_blocks(src, rows, cols):
    count = rows.shape[0]
    grid_spec = pltpu.PrefetchScalarGridSpec(
        num_scalar_prefetch=2,
        grid=(),
        in_specs=[pl.BlockSpec(memory_space=pl.ANY)],
        out_specs=pl.BlockSpec(memory_space=pl.ANY),
        scratch_shapes=[
            pltpu.VMEM(src.shape, src.dtype),
            pltpu.SemaphoreType.DMA(()),
            pltpu.SemaphoreType.DMA((count,)),
        ],
    )
    return pl.pallas_call(
        _copy_blocks,
        out_shape=jax.ShapeDtypeStruct((count, B, B), src.dtype),
        grid_spec=grid_spec,
        cost_estimate=pl.CostEstimate(
            flops=0, bytes_accessed=(src.size + count * B * B) * 4, transcendentals=0
        ),
    )(rows, cols, src)


def select_send(sigma_local, row_blocks, slots):
    own_count = lax.axis_size("own")
    own_here = lax.axis_index("own")
    row_here = lax.axis_index("row")
    rows_here = sigma_local.shape[0] // B
    cols_here = sigma_local.shape[1] // B
    rowlist = row_blocks.reshape(own_count, slots, -1)
    group = own_here * cols_here // rows_here
    want_col = lax.dynamic_index_in_dim(rowlist, group, 2, keepdims=False)
    local_col = want_col - own_here * cols_here
    match = ((local_col >= 0) & (local_col < cols_here)).astype(jnp.int32)
    which = jnp.sum(match * jnp.arange(slots, dtype=jnp.int32)[None, :], axis=1)
    chosen = rowlist[jnp.arange(own_count, dtype=jnp.int32), which]
    chosen_row = jnp.clip(
        lax.dynamic_index_in_dim(chosen, row_here, 1, keepdims=False) - row_here * rows_here,
        0,
        rows_here - 1,
    )
    chosen_col = jnp.clip(
        lax.dynamic_index_in_dim(chosen, group, 1, keepdims=False) - own_here * cols_here,
        0,
        cols_here - 1,
    )
    return gather_blocks(sigma_local, chosen_row, chosen_col)


def _take_blocks(which_ref, src_ref, out_ref, staged, sems_in, sem_out):
    count = staged.shape[0]
    copies = []
    for i in range(count):
        copy = pltpu.make_async_copy(src_ref.at[which_ref[i]], staged.at[i], sems_in.at[i])
        copy.start()
        copies.append(copy)
    for copy in copies:
        copy.wait()
    store = pltpu.make_async_copy(staged, out_ref, sem_out)
    store.start()
    store.wait()


def select_take(received, row_blocks, slots, cols_here):
    mine = lax.axis_index("own") * slots + jnp.arange(slots, dtype=jnp.int32)
    rowlist = row_blocks[mine]
    sender = jnp.clip(rowlist // cols_here, 0, received.shape[0] - 1).reshape(-1)
    count = sender.shape[0]
    grid_spec = pltpu.PrefetchScalarGridSpec(
        num_scalar_prefetch=1,
        grid=(),
        in_specs=[pl.BlockSpec(memory_space=pl.ANY)],
        out_specs=pl.BlockSpec(memory_space=pl.ANY),
        scratch_shapes=[
            pltpu.VMEM((count, B, B), received.dtype),
            pltpu.SemaphoreType.DMA((count,)),
            pltpu.SemaphoreType.DMA(()),
        ],
    )
    taken = pl.pallas_call(
        _take_blocks,
        out_shape=jax.ShapeDtypeStruct((count, B, B), received.dtype),
        grid_spec=grid_spec,
        cost_estimate=pl.CostEstimate(
            flops=0, bytes_accessed=2 * count * B * B * 4, transcendentals=0
        ),
    )(sender, received)
    return taken.reshape(slots, -1, B, B)


def on_device(
    sigma_anc, row_blocks, panel1, diag_inv1, mask1, parent_block2, panel2, diag_inv2, mask2
):
    slots = panel1.shape[0]
    cols_here = sigma_anc.shape[1] // B
    row_count = lax.axis_size("row")
    row_here = lax.axis_index("row")
    core = row_here % 2
    keep_own2 = mask2.astype(jnp.float32)
    factor2_own = keep_own2[:, :, None] * product("kij,kjc->kic", panel2, diag_inv2)
    piece = B // row_count
    up_own = lax.dynamic_slice_in_dim(parent_block2, row_here * piece, piece, axis=1)
    up_own = product("kij,kjc->kic", up_own, diag_inv2)
    payload = shifted(jnp.concatenate([factor2_own, up_own], axis=1), "own", -1)

    outgoing = select_send(sigma_anc, row_blocks, slots)
    payload, outgoing = lax.optimization_barrier((payload, outgoing))
    received = lax.all_to_all(outgoing, "own", split_axis=0, concat_axis=0, tiled=True)

    keep1 = mask1.astype(jnp.float32)
    factor1 = keep1[:, :, None] * product("kij,kjc->kic", panel1, diag_inv1)
    factor2 = keep1[:, :, None] * payload[:, :B]
    both = jnp.concatenate([factor1, factor2], axis=-1)
    boths = lax.all_gather(both, "row", axis=1, tiled=True).reshape(slots, -1, B, 2 * B)
    up_parent = lax.all_gather(payload[:, B:], "row", axis=1, tiled=True)

    blocks1 = select_take(received, row_blocks, slots, cols_here)
    kept = keep1[:, :, None] * product("kmij,kmjc->kic", blocks1, boths)
    sel1_panel = -kept[:, :, :B]
    pre2 = -(product("kij,kjc->kic", sel1_panel, up_parent) + kept[:, :, B:])
    pre2_child = shifted(pre2, "own", 1)
    terms = jnp.concatenate(
        [
            product("kji,kjc->kic", factor1, sel1_panel),
            product("kji,kjc->kic", sel1_panel, factor2),
            product("kji,kjc->kic", factor2, pre2),
        ],
        axis=-1,
    )
    summed, pre2_child = row_sum(terms, pre2_child)
    gram1 = product("kji,kjc->kic", diag_inv1, diag_inv1)
    sel1_diag = gram1 - summed[:, :, :B]
    sel2_parent = -(product("kij,kjc->kic", sel1_diag, up_parent) + summed[:, :, B : 2 * B])
    down = product("kji,kjc->kic", up_parent, sel2_parent) + summed[:, :, 2 * B :]

    partner = [(i, i ^ 1) for i in range(row_count)]
    got = shifted(jnp.where(core == 0, sel2_parent, down), "own", 1)
    other = lax.ppermute(got, "row", partner)
    sel2_parent_child = jnp.where(core == 0, got, other)
    down_child = jnp.where(core == 0, other, got)

    sel2_panel = keep_own2[:, :, None] * pre2_child
    gram2 = product("kji,kjc->kic", diag_inv2, diag_inv2)
    sel2_diag = gram2 - down_child
    return (sel1_panel, sel1_diag, sel2_parent_child, sel2_panel, sel2_diag)


def solution(mesh):
    in_specs = (
        P("row", "own"),
        P(),
        P("own", "row", None),
        P("own", None, None),
        P("own", "row"),
        P("own", None, None),
        P("own", "row", None),
        P("own", None, None),
        P("own", "row"),
    )
    out_specs = (
        P("own", "row", None),
        P("own", None, None),
        P("own", None, None),
        P("own", "row", None),
        P("own", None, None),
    )
    return jax.shard_map(
        on_device, mesh=mesh, in_specs=in_specs, out_specs=out_specs, check_vma=False
    )
```

```python
import jax
import jax.numpy as jnp
from jax import lax
from jax.experimental import pallas as pl
from jax.experimental.pallas import tpu as pltpu
from jax.sharding import PartitionSpec as P

B = 256


HIGH = lax.Precision.HIGHEST


def shifted(shard, axis, by):
    length = lax.axis_size(axis)
    return lax.ppermute(shard, axis, [(i, (i + by) % length) for i in range(length)])


def _towards(value, by):
    length = lax.axis_size("row")
    return lax.ppermute(value, "row", [(i, (i + 2 * by) % length) for i in range(length)])


def row_scatter(x):
    length = lax.axis_size("row")
    row_here = lax.axis_index("row")
    core = row_here % 2
    chip = row_here // 2
    chips = length // 2
    half = x.shape[1] // 2
    lo, hi = x[:, :half], x[:, half:]
    mine = jnp.where(core == 0, lo, hi)
    other = jnp.where(core == 0, hi, lo)
    part = mine + lax.ppermute(other, "row", [(i, i ^ 1) for i in range(length)])
    quarter = half // chips
    total = lax.dynamic_slice_in_dim(part, chip * quarter, quarter, axis=1)
    for by in range(1, chips):
        target = (chip + by) % chips
        total = total + _towards(
            lax.dynamic_slice_in_dim(part, target * quarter, quarter, axis=1), by
        )
    return total


def row_rows(piece):
    length = lax.axis_size("row")
    row_here = lax.axis_index("row")
    core = row_here % 2
    chip = row_here // 2
    chips = length // 2
    pieces = [piece] + [_towards(piece, by) for by in range(1, chips)]
    stacked = jnp.stack(pieces)
    order = (chip - jnp.arange(chips, dtype=jnp.int32)) % chips
    part = stacked[order].transpose(1, 0, 2, 3).reshape(
        piece.shape[0], chips * piece.shape[1], piece.shape[2]
    )
    got = lax.ppermute(part, "row", [(i, i ^ 1) for i in range(length)])
    return jnp.where(
        core == 0, jnp.concatenate([part, got], axis=1), jnp.concatenate([got, part], axis=1)
    )


def held_rows(x):
    length = lax.axis_size("row")
    row_here = lax.axis_index("row")
    chips = length // 2
    half = x.shape[1] // 2
    quarter = half // chips
    first = (row_here % 2) * half + (row_here // 2) * quarter
    return lax.dynamic_slice_in_dim(x, first, quarter, axis=1)


def product(form, left, right):
    return jnp.einsum(form, left, right, precision=HIGH)


def _copy_blocks(rows_ref, cols_ref, src_ref, out_ref, staged, sem_in, sems_out):
    load = pltpu.make_async_copy(src_ref, staged, sem_in)
    load.start()
    load.wait()
    count = out_ref.shape[0]
    copies = []
    for i in range(count):
        copy = pltpu.make_async_copy(
            staged.at[pl.ds(rows_ref[i] * B, B), pl.ds(pl.multiple_of(cols_ref[i] * B, B), B)],
            out_ref.at[i],
            sems_out.at[i],
        )
        copy.start()
        copies.append(copy)
    for copy in copies:
        copy.wait()


def gather_blocks(src, rows, cols):
    count = rows.shape[0]
    grid_spec = pltpu.PrefetchScalarGridSpec(
        num_scalar_prefetch=2,
        grid=(),
        in_specs=[pl.BlockSpec(memory_space=pl.ANY)],
        out_specs=pl.BlockSpec(memory_space=pl.ANY),
        scratch_shapes=[
            pltpu.VMEM(src.shape, src.dtype),
            pltpu.SemaphoreType.DMA(()),
            pltpu.SemaphoreType.DMA((count,)),
        ],
    )
    return pl.pallas_call(
        _copy_blocks,
        out_shape=jax.ShapeDtypeStruct((count, B, B), src.dtype),
        grid_spec=grid_spec,
        cost_estimate=pl.CostEstimate(
            flops=0, bytes_accessed=(src.size + count * B * B) * 4, transcendentals=0
        ),
    )(rows, cols, src)


def select_send(sigma_local, row_blocks, slots):
    own_count = lax.axis_size("own")
    own_here = lax.axis_index("own")
    row_here = lax.axis_index("row")
    rows_here = sigma_local.shape[0] // B
    cols_here = sigma_local.shape[1] // B
    rowlist = row_blocks.reshape(own_count, slots, -1)
    group = own_here * cols_here // rows_here
    want_col = lax.dynamic_index_in_dim(rowlist, group, 2, keepdims=False)
    local_col = want_col - own_here * cols_here
    match = ((local_col >= 0) & (local_col < cols_here)).astype(jnp.int32)
    which = jnp.sum(match * jnp.arange(slots, dtype=jnp.int32)[None, :], axis=1)
    chosen = rowlist[jnp.arange(own_count, dtype=jnp.int32), which]
    chosen_row = jnp.clip(
        lax.dynamic_index_in_dim(chosen, row_here, 1, keepdims=False) - row_here * rows_here,
        0,
        rows_here - 1,
    )
    chosen_col = jnp.clip(
        lax.dynamic_index_in_dim(chosen, group, 1, keepdims=False) - own_here * cols_here,
        0,
        cols_here - 1,
    )
    return gather_blocks(sigma_local, chosen_row, chosen_col)


def _take_blocks(which_ref, src_ref, out_ref, staged, sems_in, sem_out):
    count = staged.shape[0]
    copies = []
    for i in range(count):
        copy = pltpu.make_async_copy(src_ref.at[which_ref[i]], staged.at[i], sems_in.at[i])
        copy.start()
        copies.append(copy)
    for copy in copies:
        copy.wait()
    store = pltpu.make_async_copy(staged, out_ref, sem_out)
    store.start()
    store.wait()


def select_take(received, row_blocks, slots, cols_here):
    mine = lax.axis_index("own") * slots + jnp.arange(slots, dtype=jnp.int32)
    rowlist = row_blocks[mine]
    sender = jnp.clip(rowlist // cols_here, 0, received.shape[0] - 1).reshape(-1)
    count = sender.shape[0]
    grid_spec = pltpu.PrefetchScalarGridSpec(
        num_scalar_prefetch=1,
        grid=(),
        in_specs=[pl.BlockSpec(memory_space=pl.ANY)],
        out_specs=pl.BlockSpec(memory_space=pl.ANY),
        scratch_shapes=[
            pltpu.VMEM((count, B, B), received.dtype),
            pltpu.SemaphoreType.DMA((count,)),
            pltpu.SemaphoreType.DMA(()),
        ],
    )
    taken = pl.pallas_call(
        _take_blocks,
        out_shape=jax.ShapeDtypeStruct((count, B, B), received.dtype),
        grid_spec=grid_spec,
        cost_estimate=pl.CostEstimate(
            flops=0, bytes_accessed=2 * count * B * B * 4, transcendentals=0
        ),
    )(sender, received)
    return taken.reshape(slots, -1, B, B)


def on_device(
    sigma_anc, row_blocks, panel1, diag_inv1, mask1, parent_block2, panel2, diag_inv2, mask2
):
    slots = panel1.shape[0]
    cols_here = sigma_anc.shape[1] // B
    row_count = lax.axis_size("row")
    row_here = lax.axis_index("row")
    keep_own2 = mask2.astype(jnp.float32)
    factor2_own = keep_own2[:, :, None] * product("kij,kjc->kic", panel2, diag_inv2)
    piece = B // row_count
    up_own = lax.dynamic_slice_in_dim(parent_block2, row_here * piece, piece, axis=1)
    up_own = product("kij,kjc->kic", up_own, diag_inv2)
    payload = shifted(jnp.concatenate([factor2_own, up_own], axis=1), "own", -1)

    outgoing = select_send(sigma_anc, row_blocks, slots)
    payload, outgoing = lax.optimization_barrier((payload, outgoing))
    received = lax.all_to_all(outgoing, "own", split_axis=0, concat_axis=0, tiled=True)

    keep1 = mask1.astype(jnp.float32)
    factor1 = keep1[:, :, None] * product("kij,kjc->kic", panel1, diag_inv1)
    factor2 = keep1[:, :, None] * payload[:, :B]
    both = jnp.concatenate([factor1, factor2], axis=-1)
    boths = lax.all_gather(both, "row", axis=1, tiled=True).reshape(slots, -1, B, 2 * B)
    up_parent = lax.all_gather(payload[:, B:], "row", axis=1, tiled=True)

    blocks1 = select_take(received, row_blocks, slots, cols_here)
    kept = keep1[:, :, None] * product("kmij,kmjc->kic", blocks1, boths)
    sel1_panel = -kept[:, :, :B]
    pre2 = -(product("kij,kjc->kic", sel1_panel, up_parent) + kept[:, :, B:])
    pre2_child = shifted(pre2, "own", 1)
    terms = jnp.concatenate(
        [
            product("kji,kjc->kic", factor1, sel1_panel),
            product("kji,kjc->kic", sel1_panel, factor2),
            product("kji,kjc->kic", factor2, pre2),
        ],
        axis=-1,
    )
    summed = row_scatter(terms)
    pre2_child, summed = lax.optimization_barrier((pre2_child, summed))
    gram1 = product("kji,kjc->kic", diag_inv1, diag_inv1)
    diag_piece = held_rows(gram1) - summed[:, :, :B]
    parent_piece = -(product("kij,kjc->kic", diag_piece, up_parent) + summed[:, :, B : 2 * B])
    sel1_diag = row_rows(diag_piece)
    child = row_rows(
        shifted(jnp.concatenate([parent_piece, summed[:, :, 2 * B :]], axis=-1), "own", 1)
    )
    sel2_parent_child = child[:, :, :B]
    up_own_full = product("kij,kjc->kic", parent_block2, diag_inv2)

    sel2_panel = keep_own2[:, :, None] * pre2_child
    gram2 = product("kji,kjc->kic", diag_inv2, diag_inv2)
    sel2_diag = gram2 - product("kji,kjc->kic", up_own_full, sel2_parent_child) - child[:, :, B:]
    return (sel1_panel, sel1_diag, sel2_parent_child, sel2_panel, sel2_diag)


def solution(mesh):
    in_specs = (
        P("row", "own"),
        P(),
        P("own", "row", None),
        P("own", None, None),
        P("own", "row"),
        P("own", None, None),
        P("own", "row", None),
        P("own", None, None),
        P("own", "row"),
    )
    out_specs = (
        P("own", "row", None),
        P("own", None, None),
        P("own", None, None),
        P("own", "row", None),
        P("own", None, None),
    )
    return jax.shard_map(
        on_device, mesh=mesh, in_specs=in_specs, out_specs=out_specs, check_vma=False
    )
```

```python
import jax
import jax.numpy as jnp
from jax import lax
from jax.experimental import pallas as pl
from jax.experimental.pallas import tpu as pltpu
from jax.sharding import PartitionSpec as P

B = 256


HIGH = lax.Precision.HIGHEST


def shifted(shard, axis, by):
    length = lax.axis_size(axis)
    return lax.ppermute(shard, axis, [(i, (i + by) % length) for i in range(length)])


def _towards(value, by):
    length = lax.axis_size("row")
    return lax.ppermute(value, "row", [(i, (i + 2 * by) % length) for i in range(length)])


def row_scatter(x):
    length = lax.axis_size("row")
    row_here = lax.axis_index("row")
    core = row_here % 2
    chip = row_here // 2
    chips = length // 2
    half = x.shape[1] // 2
    lo, hi = x[:, :half], x[:, half:]
    mine = jnp.where(core == 0, lo, hi)
    other = jnp.where(core == 0, hi, lo)
    part = mine + lax.ppermute(other, "row", [(i, i ^ 1) for i in range(length)])
    quarter = half // chips
    total = lax.dynamic_slice_in_dim(part, chip * quarter, quarter, axis=1)
    for by in range(1, chips):
        target = (chip + by) % chips
        total = total + _towards(
            lax.dynamic_slice_in_dim(part, target * quarter, quarter, axis=1), by
        )
    return total


def row_rows(piece):
    length = lax.axis_size("row")
    row_here = lax.axis_index("row")
    core = row_here % 2
    chip = row_here // 2
    chips = length // 2
    pieces = [piece] + [_towards(piece, by) for by in range(1, chips)]
    stacked = jnp.stack(pieces)
    order = (chip - jnp.arange(chips, dtype=jnp.int32)) % chips
    part = stacked[order].transpose(1, 0, 2, 3).reshape(
        piece.shape[0], chips * piece.shape[1], piece.shape[2]
    )
    got = lax.ppermute(part, "row", [(i, i ^ 1) for i in range(length)])
    return jnp.where(
        core == 0, jnp.concatenate([part, got], axis=1), jnp.concatenate([got, part], axis=1)
    )


def row_gather(x):
    length = lax.axis_size("row")
    row_here = lax.axis_index("row")
    core = row_here % 2
    chip = row_here // 2
    chips = length // 2
    got = lax.ppermute(x, "row", [(i, i ^ 1) for i in range(length)])
    pair = jnp.where(core == 0, jnp.stack([x, got]), jnp.stack([got, x]))
    stacked = jnp.stack([pair] + [_towards(pair, by) for by in range(1, chips)])
    order = (chip - jnp.arange(chips, dtype=jnp.int32)) % chips
    return stacked[order].reshape((length,) + x.shape)


def held_rows(x):
    length = lax.axis_size("row")
    row_here = lax.axis_index("row")
    chips = length // 2
    half = x.shape[1] // 2
    quarter = half // chips
    first = (row_here % 2) * half + (row_here // 2) * quarter
    return lax.dynamic_slice_in_dim(x, first, quarter, axis=1)


def product(form, left, right):
    return jnp.einsum(form, left, right, precision=HIGH)


def _copy_blocks(rows_ref, cols_ref, src_ref, out_ref, staged, sem_in, sems_out):
    load = pltpu.make_async_copy(src_ref, staged, sem_in)
    load.start()
    load.wait()
    count = out_ref.shape[0]
    copies = []
    for i in range(count):
        copy = pltpu.make_async_copy(
            staged.at[pl.ds(rows_ref[i] * B, B), pl.ds(pl.multiple_of(cols_ref[i] * B, B), B)],
            out_ref.at[i],
            sems_out.at[i],
        )
        copy.start()
        copies.append(copy)
    for copy in copies:
        copy.wait()


def gather_blocks(src, rows, cols):
    count = rows.shape[0]
    grid_spec = pltpu.PrefetchScalarGridSpec(
        num_scalar_prefetch=2,
        grid=(),
        in_specs=[pl.BlockSpec(memory_space=pl.ANY)],
        out_specs=pl.BlockSpec(memory_space=pl.ANY),
        scratch_shapes=[
            pltpu.VMEM(src.shape, src.dtype),
            pltpu.SemaphoreType.DMA(()),
            pltpu.SemaphoreType.DMA((count,)),
        ],
    )
    return pl.pallas_call(
        _copy_blocks,
        out_shape=jax.ShapeDtypeStruct((count, B, B), src.dtype),
        grid_spec=grid_spec,
        cost_estimate=pl.CostEstimate(
            flops=0, bytes_accessed=(src.size + count * B * B) * 4, transcendentals=0
        ),
    )(rows, cols, src)


def select_send(sigma_local, row_blocks, slots):
    own_count = lax.axis_size("own")
    own_here = lax.axis_index("own")
    row_here = lax.axis_index("row")
    rows_here = sigma_local.shape[0] // B
    cols_here = sigma_local.shape[1] // B
    rowlist = row_blocks.reshape(own_count, slots, -1)
    group = own_here * cols_here // rows_here
    want_col = lax.dynamic_index_in_dim(rowlist, group, 2, keepdims=False)
    local_col = want_col - own_here * cols_here
    match = ((local_col >= 0) & (local_col < cols_here)).astype(jnp.int32)
    which = jnp.sum(match * jnp.arange(slots, dtype=jnp.int32)[None, :], axis=1)
    chosen = rowlist[jnp.arange(own_count, dtype=jnp.int32), which]
    chosen_row = jnp.clip(
        lax.dynamic_index_in_dim(chosen, row_here, 1, keepdims=False) - row_here * rows_here,
        0,
        rows_here - 1,
    )
    chosen_col = jnp.clip(
        lax.dynamic_index_in_dim(chosen, group, 1, keepdims=False) - own_here * cols_here,
        0,
        cols_here - 1,
    )
    return gather_blocks(sigma_local, chosen_row, chosen_col)


def _take_blocks(which_ref, src_ref, out_ref, staged, sems_in, sem_out):
    count = staged.shape[0]
    copies = []
    for i in range(count):
        copy = pltpu.make_async_copy(src_ref.at[which_ref[i]], staged.at[i], sems_in.at[i])
        copy.start()
        copies.append(copy)
    for copy in copies:
        copy.wait()
    store = pltpu.make_async_copy(staged, out_ref, sem_out)
    store.start()
    store.wait()


def select_take(received, row_blocks, slots, cols_here):
    mine = lax.axis_index("own") * slots + jnp.arange(slots, dtype=jnp.int32)
    rowlist = row_blocks[mine]
    sender = jnp.clip(rowlist // cols_here, 0, received.shape[0] - 1).reshape(-1)
    count = sender.shape[0]
    grid_spec = pltpu.PrefetchScalarGridSpec(
        num_scalar_prefetch=1,
        grid=(),
        in_specs=[pl.BlockSpec(memory_space=pl.ANY)],
        out_specs=pl.BlockSpec(memory_space=pl.ANY),
        scratch_shapes=[
            pltpu.VMEM((count, B, B), received.dtype),
            pltpu.SemaphoreType.DMA((count,)),
            pltpu.SemaphoreType.DMA(()),
        ],
    )
    taken = pl.pallas_call(
        _take_blocks,
        out_shape=jax.ShapeDtypeStruct((count, B, B), received.dtype),
        grid_spec=grid_spec,
        cost_estimate=pl.CostEstimate(
            flops=0, bytes_accessed=2 * count * B * B * 4, transcendentals=0
        ),
    )(sender, received)
    return taken.reshape(slots, -1, B, B)


def on_device(
    sigma_anc, row_blocks, panel1, diag_inv1, mask1, parent_block2, panel2, diag_inv2, mask2
):
    slots = panel1.shape[0]
    cols_here = sigma_anc.shape[1] // B
    row_count = lax.axis_size("row")
    row_here = lax.axis_index("row")
    keep_own2 = mask2.astype(jnp.float32)
    factor2_own = keep_own2[:, :, None] * product("kij,kjc->kic", panel2, diag_inv2)
    piece = B // row_count
    up_own = lax.dynamic_slice_in_dim(parent_block2, row_here * piece, piece, axis=1)
    up_own = product("kij,kjc->kic", up_own, diag_inv2)
    payload = shifted(jnp.concatenate([factor2_own, up_own], axis=1), "own", -1)

    outgoing = select_send(sigma_anc, row_blocks, slots)
    payload, outgoing = lax.optimization_barrier((payload, outgoing))
    received = lax.all_to_all(outgoing, "own", split_axis=0, concat_axis=0, tiled=True)

    keep1 = mask1.astype(jnp.float32)
    factor1 = keep1[:, :, None] * product("kij,kjc->kic", panel1, diag_inv1)
    factor2 = keep1[:, :, None] * payload[:, :B]
    both = jnp.concatenate([factor1, factor2], axis=-1)
    boths = row_gather(both)
    up_parent = row_gather(payload[:, B:])
    up_parent = up_parent.transpose(1, 0, 2, 3).reshape(slots, B, B)

    blocks1 = select_take(received, row_blocks, slots, cols_here)
    kept = keep1[:, :, None] * product("kmij,mkjc->kic", blocks1, boths)
    sel1_panel = -kept[:, :, :B]
    pre2 = -(product("kij,kjc->kic", sel1_panel, up_parent) + kept[:, :, B:])
    pre2_child = shifted(pre2, "own", 1)
    terms = jnp.concatenate(
        [
            product("kji,kjc->kic", factor1, sel1_panel),
            product("kji,kjc->kic", sel1_panel, factor2),
            product("kji,kjc->kic", factor2, pre2),
        ],
        axis=-1,
    )
    summed = row_scatter(terms)
    pre2_child, summed = lax.optimization_barrier((pre2_child, summed))
    gram1 = product("kji,kjc->kic", diag_inv1, diag_inv1)
    diag_piece = held_rows(gram1) - summed[:, :, :B]
    parent_piece = -(product("kij,kjc->kic", diag_piece, up_parent) + summed[:, :, B : 2 * B])
    sel1_diag = row_rows(diag_piece)
    child = row_rows(
        shifted(jnp.concatenate([parent_piece, summed[:, :, 2 * B :]], axis=-1), "own", 1)
    )
    sel2_parent_child = child[:, :, :B]
    up_own_full = product("kij,kjc->kic", parent_block2, diag_inv2)

    sel2_panel = keep_own2[:, :, None] * pre2_child
    gram2 = product("kji,kjc->kic", diag_inv2, diag_inv2)
    sel2_diag = gram2 - product("kji,kjc->kic", up_own_full, sel2_parent_child) - child[:, :, B:]
    return (sel1_panel, sel1_diag, sel2_parent_child, sel2_panel, sel2_diag)


def solution(mesh):
    in_specs = (
        P("row", "own"),
        P(),
        P("own", "row", None),
        P("own", None, None),
        P("own", "row"),
        P("own", None, None),
        P("own", "row", None),
        P("own", None, None),
        P("own", "row"),
    )
    out_specs = (
        P("own", "row", None),
        P("own", None, None),
        P("own", None, None),
        P("own", "row", None),
        P("own", None, None),
    )
    return jax.shard_map(
        on_device, mesh=mesh, in_specs=in_specs, out_specs=out_specs, check_vma=False
    )
```

```python
import jax
import jax.numpy as jnp
from jax import lax
from jax.experimental import pallas as pl
from jax.experimental.pallas import tpu as pltpu
from jax.sharding import PartitionSpec as P

B = 256


HIGH = lax.Precision.HIGHEST


def shifted(shard, axis, by):
    length = lax.axis_size(axis)
    return lax.ppermute(shard, axis, [(i, (i + by) % length) for i in range(length)])


def _towards(value, by):
    length = lax.axis_size("row")
    return lax.ppermute(value, "row", [(i, (i + 2 * by) % length) for i in range(length)])


def row_scatter(x):
    length = lax.axis_size("row")
    row_here = lax.axis_index("row")
    core = row_here % 2
    chip = row_here // 2
    chips = length // 2
    half = x.shape[1] // 2
    lo, hi = x[:, :half], x[:, half:]
    mine = jnp.where(core == 0, lo, hi)
    other = jnp.where(core == 0, hi, lo)
    part = mine + lax.ppermute(other, "row", [(i, i ^ 1) for i in range(length)])
    quarter = half // chips
    total = lax.dynamic_slice_in_dim(part, chip * quarter, quarter, axis=1)
    for by in range(1, chips):
        target = (chip + by) % chips
        total = total + _towards(
            lax.dynamic_slice_in_dim(part, target * quarter, quarter, axis=1), by
        )
    return total


def row_rows(piece):
    length = lax.axis_size("row")
    row_here = lax.axis_index("row")
    core = row_here % 2
    chip = row_here // 2
    chips = length // 2
    pieces = [piece] + [_towards(piece, by) for by in range(1, chips)]
    stacked = jnp.stack(pieces)
    order = (chip - jnp.arange(chips, dtype=jnp.int32)) % chips
    part = stacked[order].transpose(1, 0, 2, 3).reshape(
        piece.shape[0], chips * piece.shape[1], piece.shape[2]
    )
    got = lax.ppermute(part, "row", [(i, i ^ 1) for i in range(length)])
    return jnp.where(
        core == 0, jnp.concatenate([part, got], axis=1), jnp.concatenate([got, part], axis=1)
    )


def row_gather(x):
    length = lax.axis_size("row")
    row_here = lax.axis_index("row")
    core = row_here % 2
    chip = row_here // 2
    chips = length // 2
    got = lax.ppermute(x, "row", [(i, i ^ 1) for i in range(length)])
    pair = jnp.where(core == 0, jnp.stack([x, got]), jnp.stack([got, x]))
    stacked = jnp.stack([pair] + [_towards(pair, by) for by in range(1, chips)])
    order = (chip - jnp.arange(chips, dtype=jnp.int32)) % chips
    return stacked[order].reshape((length,) + x.shape)


def held_rows(x):
    length = lax.axis_size("row")
    row_here = lax.axis_index("row")
    chips = length // 2
    half = x.shape[1] // 2
    quarter = half // chips
    first = (row_here % 2) * half + (row_here // 2) * quarter
    return lax.dynamic_slice_in_dim(x, first, quarter, axis=1)


def product(form, left, right):
    return jnp.einsum(form, left, right, precision=HIGH)


def _copy_blocks(rows_ref, cols_ref, src_ref, out_ref, staged, sem_in, sems_out):
    load = pltpu.make_async_copy(src_ref, staged, sem_in)
    load.start()
    load.wait()
    count = out_ref.shape[0]
    copies = []
    for i in range(count):
        copy = pltpu.make_async_copy(
            staged.at[pl.ds(rows_ref[i] * B, B), pl.ds(pl.multiple_of(cols_ref[i] * B, B), B)],
            out_ref.at[i],
            sems_out.at[i],
        )
        copy.start()
        copies.append(copy)
    for copy in copies:
        copy.wait()


def gather_blocks(src, rows, cols):
    count = rows.shape[0]
    grid_spec = pltpu.PrefetchScalarGridSpec(
        num_scalar_prefetch=2,
        grid=(),
        in_specs=[pl.BlockSpec(memory_space=pl.ANY)],
        out_specs=pl.BlockSpec(memory_space=pl.ANY),
        scratch_shapes=[
            pltpu.VMEM(src.shape, src.dtype),
            pltpu.SemaphoreType.DMA(()),
            pltpu.SemaphoreType.DMA((count,)),
        ],
    )
    return pl.pallas_call(
        _copy_blocks,
        out_shape=jax.ShapeDtypeStruct((count, B, B), src.dtype),
        grid_spec=grid_spec,
        cost_estimate=pl.CostEstimate(
            flops=0, bytes_accessed=(src.size + count * B * B) * 4, transcendentals=0
        ),
    )(rows, cols, src)


def select_send(sigma_local, row_blocks, slots):
    own_count = lax.axis_size("own")
    own_here = lax.axis_index("own")
    row_here = lax.axis_index("row")
    rows_here = sigma_local.shape[0] // B
    cols_here = sigma_local.shape[1] // B
    rowlist = row_blocks.reshape(own_count, slots, -1)
    group = own_here * cols_here // rows_here
    want_col = lax.dynamic_index_in_dim(rowlist, group, 2, keepdims=False)
    local_col = want_col - own_here * cols_here
    match = ((local_col >= 0) & (local_col < cols_here)).astype(jnp.int32)
    which = jnp.sum(match * jnp.arange(slots, dtype=jnp.int32)[None, :], axis=1)
    chosen = rowlist[jnp.arange(own_count, dtype=jnp.int32), which]
    chosen_row = jnp.clip(
        lax.dynamic_index_in_dim(chosen, row_here, 1, keepdims=False) - row_here * rows_here,
        0,
        rows_here - 1,
    )
    chosen_col = jnp.clip(
        lax.dynamic_index_in_dim(chosen, group, 1, keepdims=False) - own_here * cols_here,
        0,
        cols_here - 1,
    )
    return gather_blocks(sigma_local, chosen_row, chosen_col)


def _take_blocks(which_ref, src_ref, out_ref, staged, sems_in, sem_out):
    count = staged.shape[0]
    copies = []
    for i in range(count):
        copy = pltpu.make_async_copy(src_ref.at[which_ref[i]], staged.at[i], sems_in.at[i])
        copy.start()
        copies.append(copy)
    for copy in copies:
        copy.wait()
    store = pltpu.make_async_copy(staged, out_ref, sem_out)
    store.start()
    store.wait()


def select_take(received, row_blocks, slots, cols_here):
    mine = lax.axis_index("own") * slots + jnp.arange(slots, dtype=jnp.int32)
    rowlist = row_blocks[mine]
    sender = jnp.clip(rowlist // cols_here, 0, received.shape[0] - 1).reshape(-1)
    count = sender.shape[0]
    grid_spec = pltpu.PrefetchScalarGridSpec(
        num_scalar_prefetch=1,
        grid=(),
        in_specs=[pl.BlockSpec(memory_space=pl.ANY)],
        out_specs=pl.BlockSpec(memory_space=pl.ANY),
        scratch_shapes=[
            pltpu.VMEM((count, B, B), received.dtype),
            pltpu.SemaphoreType.DMA((count,)),
            pltpu.SemaphoreType.DMA(()),
        ],
    )
    taken = pl.pallas_call(
        _take_blocks,
        out_shape=jax.ShapeDtypeStruct((count, B, B), received.dtype),
        grid_spec=grid_spec,
        cost_estimate=pl.CostEstimate(
            flops=0, bytes_accessed=2 * count * B * B * 4, transcendentals=0
        ),
    )(sender, received)
    return taken.reshape(slots, -1, B, B)


def _panel_product(which_ref, blocks_ref, factors_ref, out_ref, total):
    m = pl.program_id(1)

    @pl.when(m == 0)
    def _():
        total[...] = jnp.zeros_like(total)

    total[...] += jnp.dot(
        blocks_ref[0], factors_ref[0, 0], precision=HIGH, preferred_element_type=jnp.float32
    )

    @pl.when(m == pl.num_programs(1) - 1)
    def _():
        out_ref[0] = total[...]


def panel_product(received, boths, row_blocks, slots, cols_here):
    mine = lax.axis_index("own") * slots + jnp.arange(slots, dtype=jnp.int32)
    sender = jnp.clip(row_blocks[mine] // cols_here, 0, received.shape[0] - 1)
    groups = sender.shape[1]
    width = boths.shape[-1]
    grid_spec = pltpu.PrefetchScalarGridSpec(
        num_scalar_prefetch=1,
        grid=(slots, groups),
        in_specs=[
            pl.BlockSpec((1, B, B), lambda k, m, w: (w[k * groups + m], 0, 0)),
            pl.BlockSpec((1, 1, B, width), lambda k, m, w: (m, k, 0, 0)),
        ],
        out_specs=pl.BlockSpec((1, B, width), lambda k, m, w: (k, 0, 0)),
        scratch_shapes=[pltpu.VMEM((B, width), jnp.float32)],
    )
    return pl.pallas_call(
        _panel_product,
        out_shape=jax.ShapeDtypeStruct((slots, B, width), jnp.float32),
        grid_spec=grid_spec,
        cost_estimate=pl.CostEstimate(
            flops=2 * slots * groups * B * B * width,
            bytes_accessed=4 * slots * groups * (B * B + B * width),
            transcendentals=0,
        ),
    )(sender.reshape(-1), received, boths)


def on_device(
    sigma_anc, row_blocks, panel1, diag_inv1, mask1, parent_block2, panel2, diag_inv2, mask2
):
    slots = panel1.shape[0]
    cols_here = sigma_anc.shape[1] // B
    row_count = lax.axis_size("row")
    row_here = lax.axis_index("row")
    keep_own2 = mask2.astype(jnp.float32)
    factor2_own = keep_own2[:, :, None] * product("kij,kjc->kic", panel2, diag_inv2)
    piece = B // row_count
    up_own = lax.dynamic_slice_in_dim(parent_block2, row_here * piece, piece, axis=1)
    up_own = product("kij,kjc->kic", up_own, diag_inv2)
    payload = shifted(jnp.concatenate([factor2_own, up_own], axis=1), "own", -1)

    outgoing = select_send(sigma_anc, row_blocks, slots)
    payload, outgoing = lax.optimization_barrier((payload, outgoing))
    received = lax.all_to_all(outgoing, "own", split_axis=0, concat_axis=0, tiled=True)

    keep1 = mask1.astype(jnp.float32)
    factor1 = keep1[:, :, None] * product("kij,kjc->kic", panel1, diag_inv1)
    factor2 = keep1[:, :, None] * payload[:, :B]
    both = jnp.concatenate([factor1, factor2], axis=-1)
    boths = row_gather(both)
    up_parent = row_gather(payload[:, B:])
    up_parent = up_parent.transpose(1, 0, 2, 3).reshape(slots, B, B)

    kept = keep1[:, :, None] * panel_product(received, boths, row_blocks, slots, cols_here)
    sel1_panel = -kept[:, :, :B]
    pre2 = -(product("kij,kjc->kic", sel1_panel, up_parent) + kept[:, :, B:])
    pre2_child = shifted(pre2, "own", 1)
    terms = jnp.concatenate(
        [
            product("kji,kjc->kic", factor1, sel1_panel),
            product("kji,kjc->kic", sel1_panel, factor2),
            product("kji,kjc->kic", factor2, pre2),
        ],
        axis=-1,
    )
    summed = row_scatter(terms)
    pre2_child, summed = lax.optimization_barrier((pre2_child, summed))
    gram1 = product("kji,kjc->kic", diag_inv1, diag_inv1)
    diag_piece = held_rows(gram1) - summed[:, :, :B]
    parent_piece = -(product("kij,kjc->kic", diag_piece, up_parent) + summed[:, :, B : 2 * B])
    sel1_diag = row_rows(diag_piece)
    child = row_rows(
        shifted(jnp.concatenate([parent_piece, summed[:, :, 2 * B :]], axis=-1), "own", 1)
    )
    sel2_parent_child = child[:, :, :B]
    up_own_full = product("kij,kjc->kic", parent_block2, diag_inv2)

    sel2_panel = keep_own2[:, :, None] * pre2_child
    gram2 = product("kji,kjc->kic", diag_inv2, diag_inv2)
    sel2_diag = gram2 - product("kji,kjc->kic", up_own_full, sel2_parent_child) - child[:, :, B:]
    return (sel1_panel, sel1_diag, sel2_parent_child, sel2_panel, sel2_diag)


def solution(mesh):
    in_specs = (
        P("row", "own"),
        P(),
        P("own", "row", None),
        P("own", None, None),
        P("own", "row"),
        P("own", None, None),
        P("own", "row", None),
        P("own", None, None),
        P("own", "row"),
    )
    out_specs = (
        P("own", "row", None),
        P("own", None, None),
        P("own", None, None),
        P("own", "row", None),
        P("own", None, None),
    )
    return jax.shard_map(
        on_device, mesh=mesh, in_specs=in_specs, out_specs=out_specs, check_vma=False
    )
```

```python
import jax
import jax.numpy as jnp
from jax import lax
from jax.experimental import pallas as pl
from jax.experimental.pallas import tpu as pltpu
from jax.sharding import PartitionSpec as P

B = 256


HIGH = lax.Precision.HIGHEST


def shifted(shard, axis, by):
    length = lax.axis_size(axis)
    return lax.ppermute(shard, axis, [(i, (i + by) % length) for i in range(length)])


def _towards(value, by):
    length = lax.axis_size("row")
    return lax.ppermute(value, "row", [(i, (i + 2 * by) % length) for i in range(length)])


def row_scatter(x):
    length = lax.axis_size("row")
    row_here = lax.axis_index("row")
    core = row_here % 2
    chip = row_here // 2
    chips = length // 2
    half = x.shape[1] // 2
    lo, hi = x[:, :half], x[:, half:]
    mine = jnp.where(core == 0, lo, hi)
    other = jnp.where(core == 0, hi, lo)
    part = mine + lax.ppermute(other, "row", [(i, i ^ 1) for i in range(length)])
    quarter = half // chips
    total = lax.dynamic_slice_in_dim(part, chip * quarter, quarter, axis=1)
    for by in range(1, chips):
        target = (chip + by) % chips
        total = total + _towards(
            lax.dynamic_slice_in_dim(part, target * quarter, quarter, axis=1), by
        )
    return total


def row_rows(piece):
    length = lax.axis_size("row")
    row_here = lax.axis_index("row")
    core = row_here % 2
    chip = row_here // 2
    chips = length // 2
    pieces = [piece] + [_towards(piece, by) for by in range(1, chips)]
    stacked = jnp.stack(pieces)
    order = (chip - jnp.arange(chips, dtype=jnp.int32)) % chips
    part = stacked[order].transpose(1, 0, 2, 3).reshape(
        piece.shape[0], chips * piece.shape[1], piece.shape[2]
    )
    got = lax.ppermute(part, "row", [(i, i ^ 1) for i in range(length)])
    return jnp.where(
        core == 0, jnp.concatenate([part, got], axis=1), jnp.concatenate([got, part], axis=1)
    )


def row_gather(x):
    length = lax.axis_size("row")
    row_here = lax.axis_index("row")
    core = row_here % 2
    chip = row_here // 2
    chips = length // 2
    got = lax.ppermute(x, "row", [(i, i ^ 1) for i in range(length)])
    pair = jnp.where(core == 0, jnp.stack([x, got]), jnp.stack([got, x]))
    stacked = jnp.stack([pair] + [_towards(pair, by) for by in range(1, chips)])
    order = (chip - jnp.arange(chips, dtype=jnp.int32)) % chips
    return stacked[order].reshape((length,) + x.shape)


def held_rows(x):
    length = lax.axis_size("row")
    row_here = lax.axis_index("row")
    chips = length // 2
    half = x.shape[1] // 2
    quarter = half // chips
    first = (row_here % 2) * half + (row_here // 2) * quarter
    return lax.dynamic_slice_in_dim(x, first, quarter, axis=1)


def product(form, left, right):
    return jnp.einsum(form, left, right, precision=HIGH)


def _copy_blocks(rows_ref, cols_ref, src_ref, out_ref, staged, sem_in, sems_out):
    load = pltpu.make_async_copy(src_ref, staged, sem_in)
    load.start()
    load.wait()
    count = out_ref.shape[0]
    copies = []
    for i in range(count):
        copy = pltpu.make_async_copy(
            staged.at[pl.ds(rows_ref[i] * B, B), pl.ds(pl.multiple_of(cols_ref[i] * B, B), B)],
            out_ref.at[i],
            sems_out.at[i],
        )
        copy.start()
        copies.append(copy)
    for copy in copies:
        copy.wait()


def gather_blocks(src, rows, cols):
    count = rows.shape[0]
    grid_spec = pltpu.PrefetchScalarGridSpec(
        num_scalar_prefetch=2,
        grid=(),
        in_specs=[pl.BlockSpec(memory_space=pl.ANY)],
        out_specs=pl.BlockSpec(memory_space=pl.ANY),
        scratch_shapes=[
            pltpu.VMEM(src.shape, src.dtype),
            pltpu.SemaphoreType.DMA(()),
            pltpu.SemaphoreType.DMA((count,)),
        ],
    )
    return pl.pallas_call(
        _copy_blocks,
        out_shape=jax.ShapeDtypeStruct((count, B, B), src.dtype),
        grid_spec=grid_spec,
        cost_estimate=pl.CostEstimate(
            flops=0, bytes_accessed=(src.size + count * B * B) * 4, transcendentals=0
        ),
    )(rows, cols, src)


def select_send(sigma_local, row_blocks, slots):
    own_count = lax.axis_size("own")
    own_here = lax.axis_index("own")
    row_here = lax.axis_index("row")
    rows_here = sigma_local.shape[0] // B
    cols_here = sigma_local.shape[1] // B
    rowlist = row_blocks.reshape(own_count, slots, -1)
    group = own_here * cols_here // rows_here
    want_col = lax.dynamic_index_in_dim(rowlist, group, 2, keepdims=False)
    local_col = want_col - own_here * cols_here
    match = ((local_col >= 0) & (local_col < cols_here)).astype(jnp.int32)
    which = jnp.sum(match * jnp.arange(slots, dtype=jnp.int32)[None, :], axis=1)
    chosen = rowlist[jnp.arange(own_count, dtype=jnp.int32), which]
    chosen_row = jnp.clip(
        lax.dynamic_index_in_dim(chosen, row_here, 1, keepdims=False) - row_here * rows_here,
        0,
        rows_here - 1,
    )
    chosen_col = jnp.clip(
        lax.dynamic_index_in_dim(chosen, group, 1, keepdims=False) - own_here * cols_here,
        0,
        cols_here - 1,
    )
    return gather_blocks(sigma_local, chosen_row, chosen_col)


def _take_blocks(which_ref, src_ref, out_ref, sems):
    count = out_ref.shape[0]
    copies = []
    for i in range(count):
        copy = pltpu.make_async_copy(src_ref.at[which_ref[i]], out_ref.at[i], sems.at[i])
        copy.start()
        copies.append(copy)
    for copy in copies:
        copy.wait()


def select_take(received, row_blocks, slots, cols_here):
    mine = lax.axis_index("own") * slots + jnp.arange(slots, dtype=jnp.int32)
    rowlist = row_blocks[mine]
    sender = jnp.clip(rowlist // cols_here, 0, received.shape[0] - 1).reshape(-1)
    count = sender.shape[0]
    grid_spec = pltpu.PrefetchScalarGridSpec(
        num_scalar_prefetch=1,
        grid=(),
        in_specs=[pl.BlockSpec(memory_space=pl.ANY)],
        out_specs=pl.BlockSpec(memory_space=pl.ANY),
        scratch_shapes=[pltpu.SemaphoreType.DMA((count,))],
    )
    taken = pl.pallas_call(
        _take_blocks,
        out_shape=jax.ShapeDtypeStruct((count, B, B), received.dtype),
        grid_spec=grid_spec,
        cost_estimate=pl.CostEstimate(
            flops=0, bytes_accessed=2 * count * B * B * 4, transcendentals=0
        ),
    )(sender, received)
    return taken.reshape(slots, -1, B, B)


def on_device(
    sigma_anc, row_blocks, panel1, diag_inv1, mask1, parent_block2, panel2, diag_inv2, mask2
):
    slots = panel1.shape[0]
    cols_here = sigma_anc.shape[1] // B
    row_count = lax.axis_size("row")
    row_here = lax.axis_index("row")
    keep_own2 = mask2.astype(jnp.float32)
    factor2_own = keep_own2[:, :, None] * product("kij,kjc->kic", panel2, diag_inv2)
    piece = B // row_count
    up_own = lax.dynamic_slice_in_dim(parent_block2, row_here * piece, piece, axis=1)
    up_own = product("kij,kjc->kic", up_own, diag_inv2)
    payload = shifted(jnp.concatenate([factor2_own, up_own], axis=1), "own", -1)

    outgoing = select_send(sigma_anc, row_blocks, slots)
    payload, outgoing = lax.optimization_barrier((payload, outgoing))
    received = lax.all_to_all(outgoing, "own", split_axis=0, concat_axis=0, tiled=True)

    keep1 = mask1.astype(jnp.float32)
    factor1 = keep1[:, :, None] * product("kij,kjc->kic", panel1, diag_inv1)
    factor2 = keep1[:, :, None] * payload[:, :B]
    both = jnp.concatenate([factor1, factor2], axis=-1)
    boths = row_gather(both)
    up_parent = row_gather(payload[:, B:])
    up_parent = up_parent.transpose(1, 0, 2, 3).reshape(slots, B, B)

    blocks1 = select_take(received, row_blocks, slots, cols_here)
    kept = keep1[:, :, None] * product("kmij,mkjc->kic", blocks1, boths)
    sel1_panel = -kept[:, :, :B]
    pre2 = -(product("kij,kjc->kic", sel1_panel, up_parent) + kept[:, :, B:])
    pre2_child = shifted(pre2, "own", 1)
    terms = jnp.concatenate(
        [
            product("kji,kjc->kic", factor1, sel1_panel),
            product("kji,kjc->kic", sel1_panel, factor2),
            product("kji,kjc->kic", factor2, pre2),
        ],
        axis=-1,
    )
    summed = row_scatter(terms)
    pre2_child, summed = lax.optimization_barrier((pre2_child, summed))
    gram1 = product("kji,kjc->kic", diag_inv1, diag_inv1)
    diag_piece = held_rows(gram1) - summed[:, :, :B]
    parent_piece = -(product("kij,kjc->kic", diag_piece, up_parent) + summed[:, :, B : 2 * B])
    sel1_diag = row_rows(diag_piece)
    child = row_rows(
        shifted(jnp.concatenate([parent_piece, summed[:, :, 2 * B :]], axis=-1), "own", 1)
    )
    sel2_parent_child = child[:, :, :B]
    up_own_full = product("kij,kjc->kic", parent_block2, diag_inv2)

    sel2_panel = keep_own2[:, :, None] * pre2_child
    gram2 = product("kji,kjc->kic", diag_inv2, diag_inv2)
    sel2_diag = gram2 - product("kji,kjc->kic", up_own_full, sel2_parent_child) - child[:, :, B:]
    return (sel1_panel, sel1_diag, sel2_parent_child, sel2_panel, sel2_diag)


def solution(mesh):
    in_specs = (
        P("row", "own"),
        P(),
        P("own", "row", None),
        P("own", None, None),
        P("own", "row"),
        P("own", None, None),
        P("own", "row", None),
        P("own", None, None),
        P("own", "row"),
    )
    out_specs = (
        P("own", "row", None),
        P("own", None, None),
        P("own", None, None),
        P("own", "row", None),
        P("own", None, None),
    )
    return jax.shard_map(
        on_device, mesh=mesh, in_specs=in_specs, out_specs=out_specs, check_vma=False
    )
```

```python
import jax
import jax.numpy as jnp
from jax import lax
from jax.experimental import pallas as pl
from jax.experimental.pallas import tpu as pltpu
from jax.sharding import PartitionSpec as P

B = 256


HIGH = lax.Precision.HIGHEST


def shifted(shard, axis, by):
    length = lax.axis_size(axis)
    return lax.ppermute(shard, axis, [(i, (i + by) % length) for i in range(length)])


def _towards(value, by):
    length = lax.axis_size("row")
    return lax.ppermute(value, "row", [(i, (i + 2 * by) % length) for i in range(length)])


def row_scatter(x):
    length = lax.axis_size("row")
    row_here = lax.axis_index("row")
    core = row_here % 2
    chip = row_here // 2
    chips = length // 2
    half = x.shape[1] // 2
    lo, hi = x[:, :half], x[:, half:]
    mine = jnp.where(core == 0, lo, hi)
    other = jnp.where(core == 0, hi, lo)
    part = mine + lax.ppermute(other, "row", [(i, i ^ 1) for i in range(length)])
    quarter = half // chips
    total = lax.dynamic_slice_in_dim(part, chip * quarter, quarter, axis=1)
    for by in range(1, chips):
        target = (chip + by) % chips
        total = total + _towards(
            lax.dynamic_slice_in_dim(part, target * quarter, quarter, axis=1), by
        )
    return total


def row_rows(piece):
    length = lax.axis_size("row")
    row_here = lax.axis_index("row")
    core = row_here % 2
    chip = row_here // 2
    chips = length // 2
    pieces = [piece] + [_towards(piece, by) for by in range(1, chips)]
    stacked = jnp.stack(pieces)
    order = (chip - jnp.arange(chips, dtype=jnp.int32)) % chips
    part = stacked[order].transpose(1, 0, 2, 3).reshape(
        piece.shape[0], chips * piece.shape[1], piece.shape[2]
    )
    got = lax.ppermute(part, "row", [(i, i ^ 1) for i in range(length)])
    return jnp.where(
        core == 0, jnp.concatenate([part, got], axis=1), jnp.concatenate([got, part], axis=1)
    )


def row_gather(x):
    length = lax.axis_size("row")
    row_here = lax.axis_index("row")
    core = row_here % 2
    chip = row_here // 2
    chips = length // 2
    got = lax.ppermute(x, "row", [(i, i ^ 1) for i in range(length)])
    pair = jnp.where(core == 0, jnp.stack([x, got]), jnp.stack([got, x]))
    stacked = jnp.stack([pair] + [_towards(pair, by) for by in range(1, chips)])
    order = (chip - jnp.arange(chips, dtype=jnp.int32)) % chips
    return stacked[order].reshape((length,) + x.shape)


def held_rows(x):
    length = lax.axis_size("row")
    row_here = lax.axis_index("row")
    chips = length // 2
    half = x.shape[1] // 2
    quarter = half // chips
    first = (row_here % 2) * half + (row_here // 2) * quarter
    return lax.dynamic_slice_in_dim(x, first, quarter, axis=1)


def product(form, left, right):
    return jnp.einsum(form, left, right, precision=HIGH)


def _copy_blocks(rows_ref, cols_ref, src_ref, out_ref, staged, sem_in, sems_out):
    load = pltpu.make_async_copy(src_ref, staged, sem_in)
    load.start()
    load.wait()
    count = out_ref.shape[0]
    copies = []
    for i in range(count):
        copy = pltpu.make_async_copy(
            staged.at[pl.ds(rows_ref[i] * B, B), pl.ds(pl.multiple_of(cols_ref[i] * B, B), B)],
            out_ref.at[i],
            sems_out.at[i],
        )
        copy.start()
        copies.append(copy)
    for copy in copies:
        copy.wait()


def gather_blocks(src, rows, cols):
    count = rows.shape[0]
    grid_spec = pltpu.PrefetchScalarGridSpec(
        num_scalar_prefetch=2,
        grid=(),
        in_specs=[pl.BlockSpec(memory_space=pl.ANY)],
        out_specs=pl.BlockSpec(memory_space=pl.ANY),
        scratch_shapes=[
            pltpu.VMEM(src.shape, src.dtype),
            pltpu.SemaphoreType.DMA(()),
            pltpu.SemaphoreType.DMA((count,)),
        ],
    )
    return pl.pallas_call(
        _copy_blocks,
        out_shape=jax.ShapeDtypeStruct((count, B, B), src.dtype),
        grid_spec=grid_spec,
        cost_estimate=pl.CostEstimate(
            flops=0, bytes_accessed=(src.size + count * B * B) * 4, transcendentals=0
        ),
    )(rows, cols, src)


def select_send(sigma_local, row_blocks, slots):
    own_count = lax.axis_size("own")
    own_here = lax.axis_index("own")
    row_here = lax.axis_index("row")
    rows_here = sigma_local.shape[0] // B
    cols_here = sigma_local.shape[1] // B
    rowlist = row_blocks.reshape(own_count, slots, -1)
    group = own_here * cols_here // rows_here
    want_col = lax.dynamic_index_in_dim(rowlist, group, 2, keepdims=False)
    local_col = want_col - own_here * cols_here
    match = ((local_col >= 0) & (local_col < cols_here)).astype(jnp.int32)
    which = jnp.sum(match * jnp.arange(slots, dtype=jnp.int32)[None, :], axis=1)
    chosen = rowlist[jnp.arange(own_count, dtype=jnp.int32), which]
    chosen_row = jnp.clip(
        lax.dynamic_index_in_dim(chosen, row_here, 1, keepdims=False) - row_here * rows_here,
        0,
        rows_here - 1,
    )
    chosen_col = jnp.clip(
        lax.dynamic_index_in_dim(chosen, group, 1, keepdims=False) - own_here * cols_here,
        0,
        cols_here - 1,
    )
    return gather_blocks(sigma_local, chosen_row, chosen_col)


def _take_blocks(which_ref, src_ref, out_ref, staged, sems_in, sem_out):
    count = staged.shape[0]
    copies = []
    for i in range(count):
        copy = pltpu.make_async_copy(src_ref.at[which_ref[i]], staged.at[i], sems_in.at[i])
        copy.start()
        copies.append(copy)
    for copy in copies:
        copy.wait()
    store = pltpu.make_async_copy(staged, out_ref, sem_out)
    store.start()
    store.wait()


def select_take(received, row_blocks, slots, cols_here):
    mine = lax.axis_index("own") * slots + jnp.arange(slots, dtype=jnp.int32)
    rowlist = row_blocks[mine]
    sender = jnp.clip(rowlist // cols_here, 0, received.shape[0] - 1).reshape(-1)
    count = sender.shape[0]
    grid_spec = pltpu.PrefetchScalarGridSpec(
        num_scalar_prefetch=1,
        grid=(),
        in_specs=[pl.BlockSpec(memory_space=pl.ANY)],
        out_specs=pl.BlockSpec(memory_space=pl.ANY),
        scratch_shapes=[
            pltpu.VMEM((count, B, B), received.dtype),
            pltpu.SemaphoreType.DMA((count,)),
            pltpu.SemaphoreType.DMA(()),
        ],
    )
    taken = pl.pallas_call(
        _take_blocks,
        out_shape=jax.ShapeDtypeStruct((count, B, B), received.dtype),
        grid_spec=grid_spec,
        cost_estimate=pl.CostEstimate(
            flops=0, bytes_accessed=2 * count * B * B * 4, transcendentals=0
        ),
    )(sender, received)
    return taken.reshape(slots, -1, B, B)


def on_device(
    sigma_anc, row_blocks, panel1, diag_inv1, mask1, parent_block2, panel2, diag_inv2, mask2
):
    slots = panel1.shape[0]
    cols_here = sigma_anc.shape[1] // B
    row_count = lax.axis_size("row")
    row_here = lax.axis_index("row")
    keep_own2 = mask2.astype(jnp.float32)
    factor2_own = keep_own2[:, :, None] * product("kij,kjc->kic", panel2, diag_inv2)
    piece = B // row_count
    up_own = lax.dynamic_slice_in_dim(parent_block2, row_here * piece, piece, axis=1)
    up_own = product("kij,kjc->kic", up_own, diag_inv2)
    factor2_child = shifted(factor2_own, "own", -1)
    up_child = shifted(up_own, "own", -1)

    outgoing = select_send(sigma_anc, row_blocks, slots)
    factor2_child, up_child, outgoing = lax.optimization_barrier(
        (factor2_child, up_child, outgoing)
    )
    received = lax.all_to_all(outgoing, "own", split_axis=0, concat_axis=0, tiled=True)

    keep1 = mask1.astype(jnp.float32)
    factor1 = keep1[:, :, None] * product("kij,kjc->kic", panel1, diag_inv1)
    factor2 = keep1[:, :, None] * factor2_child
    both = jnp.concatenate([factor1, factor2], axis=-1)
    boths = row_gather(both)
    up_parent = row_gather(up_child)
    up_parent = up_parent.transpose(1, 0, 2, 3).reshape(slots, B, B)

    blocks1 = select_take(received, row_blocks, slots, cols_here)
    kept = keep1[:, :, None] * product("kmij,mkjc->kic", blocks1, boths)
    sel1_panel = -kept[:, :, :B]
    pre2 = -(product("kij,kjc->kic", sel1_panel, up_parent) + kept[:, :, B:])
    pre2_child = shifted(pre2, "own", 1)
    terms = jnp.concatenate(
        [
            product("kji,kjc->kic", factor1, sel1_panel),
            product("kji,kjc->kic", sel1_panel, factor2),
            product("kji,kjc->kic", factor2, pre2),
        ],
        axis=-1,
    )
    summed = row_scatter(terms)
    pre2_child, summed = lax.optimization_barrier((pre2_child, summed))
    gram1 = product("kji,kjc->kic", diag_inv1, diag_inv1)
    diag_piece = held_rows(gram1) - summed[:, :, :B]
    parent_piece = -(product("kij,kjc->kic", diag_piece, up_parent) + summed[:, :, B : 2 * B])
    sel1_diag = row_rows(diag_piece)
    child = row_rows(
        shifted(jnp.concatenate([parent_piece, summed[:, :, 2 * B :]], axis=-1), "own", 1)
    )
    sel2_parent_child = child[:, :, :B]
    up_own_full = product("kij,kjc->kic", parent_block2, diag_inv2)

    sel2_panel = keep_own2[:, :, None] * pre2_child
    gram2 = product("kji,kjc->kic", diag_inv2, diag_inv2)
    sel2_diag = gram2 - product("kji,kjc->kic", up_own_full, sel2_parent_child) - child[:, :, B:]
    return (sel1_panel, sel1_diag, sel2_parent_child, sel2_panel, sel2_diag)


def solution(mesh):
    in_specs = (
        P("row", "own"),
        P(),
        P("own", "row", None),
        P("own", None, None),
        P("own", "row"),
        P("own", None, None),
        P("own", "row", None),
        P("own", None, None),
        P("own", "row"),
    )
    out_specs = (
        P("own", "row", None),
        P("own", None, None),
        P("own", None, None),
        P("own", "row", None),
        P("own", None, None),
    )
    return jax.shard_map(
        on_device, mesh=mesh, in_specs=in_specs, out_specs=out_specs, check_vma=False
    )
```

```python
import jax
import jax.numpy as jnp
from jax import lax
from jax.experimental import pallas as pl
from jax.experimental.pallas import tpu as pltpu
from jax.sharding import PartitionSpec as P

B = 256


HIGH = lax.Precision.HIGHEST


def shifted(shard, axis, by):
    length = lax.axis_size(axis)
    return lax.ppermute(shard, axis, [(i, (i + by) % length) for i in range(length)])


def _towards(value, by):
    length = lax.axis_size("row")
    return lax.ppermute(value, "row", [(i, (i + 2 * by) % length) for i in range(length)])


def row_scatter(x):
    length = lax.axis_size("row")
    row_here = lax.axis_index("row")
    core = row_here % 2
    chip = row_here // 2
    chips = length // 2
    half = x.shape[1] // 2
    lo, hi = x[:, :half], x[:, half:]
    mine = jnp.where(core == 0, lo, hi)
    other = jnp.where(core == 0, hi, lo)
    part = mine + lax.ppermute(other, "row", [(i, i ^ 1) for i in range(length)])
    quarter = half // chips
    total = lax.dynamic_slice_in_dim(part, chip * quarter, quarter, axis=1)
    for by in range(1, chips):
        target = (chip + by) % chips
        total = total + _towards(
            lax.dynamic_slice_in_dim(part, target * quarter, quarter, axis=1), by
        )
    return total


def row_rows(piece):
    length = lax.axis_size("row")
    row_here = lax.axis_index("row")
    core = row_here % 2
    chip = row_here // 2
    chips = length // 2
    pieces = [piece] + [_towards(piece, by) for by in range(1, chips)]
    stacked = jnp.stack(pieces)
    order = (chip - jnp.arange(chips, dtype=jnp.int32)) % chips
    part = stacked[order].transpose(1, 0, 2, 3).reshape(
        piece.shape[0], chips * piece.shape[1], piece.shape[2]
    )
    got = lax.ppermute(part, "row", [(i, i ^ 1) for i in range(length)])
    return jnp.where(
        core == 0, jnp.concatenate([part, got], axis=1), jnp.concatenate([got, part], axis=1)
    )


def row_gather(x):
    length = lax.axis_size("row")
    row_here = lax.axis_index("row")
    core = row_here % 2
    chip = row_here // 2
    chips = length // 2
    got = lax.ppermute(x, "row", [(i, i ^ 1) for i in range(length)])
    pair = jnp.where(core == 0, jnp.stack([x, got]), jnp.stack([got, x]))
    stacked = jnp.stack([pair] + [_towards(pair, by) for by in range(1, chips)])
    order = (chip - jnp.arange(chips, dtype=jnp.int32)) % chips
    return stacked[order].reshape((length,) + x.shape)


def held_rows(x):
    length = lax.axis_size("row")
    row_here = lax.axis_index("row")
    chips = length // 2
    half = x.shape[1] // 2
    quarter = half // chips
    first = (row_here % 2) * half + (row_here // 2) * quarter
    return lax.dynamic_slice_in_dim(x, first, quarter, axis=1)


def product(form, left, right):
    return jnp.einsum(form, left, right, precision=HIGH)


def _copy_blocks(rows_ref, cols_ref, src_ref, out_ref, staged, sem_in, sems_out):
    load = pltpu.make_async_copy(src_ref, staged, sem_in)
    load.start()
    load.wait()
    count = out_ref.shape[0]
    copies = []
    for i in range(count):
        copy = pltpu.make_async_copy(
            staged.at[pl.ds(rows_ref[i] * B, B), pl.ds(pl.multiple_of(cols_ref[i] * B, B), B)],
            out_ref.at[i],
            sems_out.at[i],
        )
        copy.start()
        copies.append(copy)
    for copy in copies:
        copy.wait()


def gather_blocks(src, rows, cols):
    count = rows.shape[0]
    grid_spec = pltpu.PrefetchScalarGridSpec(
        num_scalar_prefetch=2,
        grid=(),
        in_specs=[pl.BlockSpec(memory_space=pl.ANY)],
        out_specs=pl.BlockSpec(memory_space=pl.ANY),
        scratch_shapes=[
            pltpu.VMEM(src.shape, src.dtype),
            pltpu.SemaphoreType.DMA(()),
            pltpu.SemaphoreType.DMA((count,)),
        ],
    )
    return pl.pallas_call(
        _copy_blocks,
        out_shape=jax.ShapeDtypeStruct((count, B, B), src.dtype),
        grid_spec=grid_spec,
        cost_estimate=pl.CostEstimate(
            flops=0, bytes_accessed=(src.size + count * B * B) * 4, transcendentals=0
        ),
    )(rows, cols, src)


def select_send(sigma_local, row_blocks, slots):
    own_count = lax.axis_size("own")
    own_here = lax.axis_index("own")
    row_here = lax.axis_index("row")
    rows_here = sigma_local.shape[0] // B
    cols_here = sigma_local.shape[1] // B
    rowlist = row_blocks.reshape(own_count, slots, -1)
    group = own_here * cols_here // rows_here
    want_col = lax.dynamic_index_in_dim(rowlist, group, 2, keepdims=False)
    local_col = want_col - own_here * cols_here
    match = ((local_col >= 0) & (local_col < cols_here)).astype(jnp.int32)
    which = jnp.sum(match * jnp.arange(slots, dtype=jnp.int32)[None, :], axis=1)
    chosen = rowlist[jnp.arange(own_count, dtype=jnp.int32), which]
    chosen_row = jnp.clip(
        lax.dynamic_index_in_dim(chosen, row_here, 1, keepdims=False) - row_here * rows_here,
        0,
        rows_here - 1,
    )
    chosen_col = jnp.clip(
        lax.dynamic_index_in_dim(chosen, group, 1, keepdims=False) - own_here * cols_here,
        0,
        cols_here - 1,
    )
    return gather_blocks(sigma_local, chosen_row, chosen_col)


def _take_blocks(which_ref, src_ref, out_ref, staged, sems_in, sem_out):
    count = staged.shape[0]
    copies = []
    for i in range(count):
        copy = pltpu.make_async_copy(src_ref.at[which_ref[i]], staged.at[i], sems_in.at[i])
        copy.start()
        copies.append(copy)
    for copy in copies:
        copy.wait()
    store = pltpu.make_async_copy(staged, out_ref, sem_out)
    store.start()
    store.wait()


def select_take(received, row_blocks, slots, cols_here):
    mine = lax.axis_index("own") * slots + jnp.arange(slots, dtype=jnp.int32)
    rowlist = row_blocks[mine]
    sender = jnp.clip(rowlist // cols_here, 0, received.shape[0] - 1).reshape(-1)
    count = sender.shape[0]
    grid_spec = pltpu.PrefetchScalarGridSpec(
        num_scalar_prefetch=1,
        grid=(),
        in_specs=[pl.BlockSpec(memory_space=pl.ANY)],
        out_specs=pl.BlockSpec(memory_space=pl.ANY),
        scratch_shapes=[
            pltpu.VMEM((count, B, B), received.dtype),
            pltpu.SemaphoreType.DMA((count,)),
            pltpu.SemaphoreType.DMA(()),
        ],
    )
    taken = pl.pallas_call(
        _take_blocks,
        out_shape=jax.ShapeDtypeStruct((count, B, B), received.dtype),
        grid_spec=grid_spec,
        cost_estimate=pl.CostEstimate(
            flops=0, bytes_accessed=2 * count * B * B * 4, transcendentals=0
        ),
    )(sender, received)
    return taken.reshape(slots, -1, B, B)


def on_device(
    sigma_anc, row_blocks, panel1, diag_inv1, mask1, parent_block2, panel2, diag_inv2, mask2
):
    slots = panel1.shape[0]
    cols_here = sigma_anc.shape[1] // B
    row_count = lax.axis_size("row")
    row_here = lax.axis_index("row")
    keep_own2 = mask2.astype(jnp.float32)
    piece = B // row_count
    diag2_own = lax.dynamic_slice_in_dim(diag_inv2, row_here * piece, piece, axis=1)
    top2_own = lax.dynamic_slice_in_dim(parent_block2, row_here * piece, piece, axis=1)
    payload = shifted(
        jnp.concatenate([keep_own2[:, :, None] * panel2, diag2_own, top2_own], axis=1), "own", -1
    )

    outgoing = select_send(sigma_anc, row_blocks, slots)
    payload, outgoing = lax.optimization_barrier((payload, outgoing))
    received = lax.all_to_all(outgoing, "own", split_axis=0, concat_axis=0, tiled=True)

    keep1 = mask1.astype(jnp.float32)
    factor1 = keep1[:, :, None] * product("kij,kjc->kic", panel1, diag_inv1)
    diag2_child = row_gather(payload[:, B : B + piece])
    diag2_child = diag2_child.transpose(1, 0, 2, 3).reshape(slots, B, B)
    factor2 = keep1[:, :, None] * product("kij,kjc->kic", payload[:, :B], diag2_child)
    up_rows = product("kij,kjc->kic", payload[:, B + piece :], diag2_child)
    both = jnp.concatenate([factor1, factor2], axis=-1)
    boths = row_gather(both)
    up_parent = row_gather(up_rows)
    up_parent = up_parent.transpose(1, 0, 2, 3).reshape(slots, B, B)

    blocks1 = select_take(received, row_blocks, slots, cols_here)
    kept = keep1[:, :, None] * product("kmij,mkjc->kic", blocks1, boths)
    sel1_panel = -kept[:, :, :B]
    pre2 = -(product("kij,kjc->kic", sel1_panel, up_parent) + kept[:, :, B:])
    pre2_child = shifted(pre2, "own", 1)
    terms = jnp.concatenate(
        [
            product("kji,kjc->kic", factor1, sel1_panel),
            product("kji,kjc->kic", sel1_panel, factor2),
            product("kji,kjc->kic", factor2, pre2),
        ],
        axis=-1,
    )
    summed = row_scatter(terms)
    pre2_child, summed = lax.optimization_barrier((pre2_child, summed))
    gram1 = product("kji,kjc->kic", diag_inv1, diag_inv1)
    diag_piece = held_rows(gram1) - summed[:, :, :B]
    parent_piece = -(product("kij,kjc->kic", diag_piece, up_parent) + summed[:, :, B : 2 * B])
    sel1_diag = row_rows(diag_piece)
    child = row_rows(
        shifted(jnp.concatenate([parent_piece, summed[:, :, 2 * B :]], axis=-1), "own", 1)
    )
    sel2_parent_child = child[:, :, :B]
    up_own_full = product("kij,kjc->kic", parent_block2, diag_inv2)

    sel2_panel = keep_own2[:, :, None] * pre2_child
    gram2 = product("kji,kjc->kic", diag_inv2, diag_inv2)
    sel2_diag = gram2 - product("kji,kjc->kic", up_own_full, sel2_parent_child) - child[:, :, B:]
    return (sel1_panel, sel1_diag, sel2_parent_child, sel2_panel, sel2_diag)


def solution(mesh):
    in_specs = (
        P("row", "own"),
        P(),
        P("own", "row", None),
        P("own", None, None),
        P("own", "row"),
        P("own", None, None),
        P("own", "row", None),
        P("own", None, None),
        P("own", "row"),
    )
    out_specs = (
        P("own", "row", None),
        P("own", None, None),
        P("own", None, None),
        P("own", "row", None),
        P("own", None, None),
    )
    return jax.shard_map(
        on_device, mesh=mesh, in_specs=in_specs, out_specs=out_specs, check_vma=False
    )
```

```python
import jax
import jax.numpy as jnp
from jax import lax
from jax.experimental import pallas as pl
from jax.experimental.pallas import tpu as pltpu
from jax.sharding import PartitionSpec as P

B = 256


HIGH = lax.Precision.HIGHEST


def shifted(shard, axis, by):
    length = lax.axis_size(axis)
    return lax.ppermute(shard, axis, [(i, (i + by) % length) for i in range(length)])


def _towards(value, by):
    length = lax.axis_size("row")
    return lax.ppermute(value, "row", [(i, (i + 2 * by) % length) for i in range(length)])


def row_scatter(x):
    length = lax.axis_size("row")
    row_here = lax.axis_index("row")
    core = row_here % 2
    chip = row_here // 2
    chips = length // 2
    half = x.shape[1] // 2
    lo, hi = x[:, :half], x[:, half:]
    mine = jnp.where(core == 0, lo, hi)
    other = jnp.where(core == 0, hi, lo)
    part = mine + lax.ppermute(other, "row", [(i, i ^ 1) for i in range(length)])
    quarter = half // chips
    total = lax.dynamic_slice_in_dim(part, chip * quarter, quarter, axis=1)
    for by in range(1, chips):
        target = (chip + by) % chips
        total = total + _towards(
            lax.dynamic_slice_in_dim(part, target * quarter, quarter, axis=1), by
        )
    return total


def row_rows(piece):
    length = lax.axis_size("row")
    row_here = lax.axis_index("row")
    core = row_here % 2
    chip = row_here // 2
    chips = length // 2
    pieces = [piece] + [_towards(piece, by) for by in range(1, chips)]
    stacked = jnp.stack(pieces)
    order = (chip - jnp.arange(chips, dtype=jnp.int32)) % chips
    part = stacked[order].transpose(1, 0, 2, 3).reshape(
        piece.shape[0], chips * piece.shape[1], piece.shape[2]
    )
    got = lax.ppermute(part, "row", [(i, i ^ 1) for i in range(length)])
    half = part.shape[1]
    full = jnp.zeros((part.shape[0], 2 * half, part.shape[2]), part.dtype)
    full = lax.dynamic_update_slice_in_dim(full, part, core * half, axis=1)
    return lax.dynamic_update_slice_in_dim(full, got, (1 - core) * half, axis=1)


def row_gather(x):
    length = lax.axis_size("row")
    row_here = lax.axis_index("row")
    core = row_here % 2
    chip = row_here // 2
    chips = length // 2
    got = lax.ppermute(x, "row", [(i, i ^ 1) for i in range(length)])
    pair = jnp.where(core == 0, jnp.stack([x, got]), jnp.stack([got, x]))
    stacked = jnp.stack([pair] + [_towards(pair, by) for by in range(1, chips)])
    order = (chip - jnp.arange(chips, dtype=jnp.int32)) % chips
    return stacked[order].reshape((length,) + x.shape)


def held_rows(x):
    length = lax.axis_size("row")
    row_here = lax.axis_index("row")
    chips = length // 2
    half = x.shape[1] // 2
    quarter = half // chips
    first = (row_here % 2) * half + (row_here // 2) * quarter
    return lax.dynamic_slice_in_dim(x, first, quarter, axis=1)


def product(form, left, right):
    return jnp.einsum(form, left, right, precision=HIGH)


def _copy_blocks(rows_ref, cols_ref, src_ref, out_ref, staged, sem_in, sems_out):
    load = pltpu.make_async_copy(src_ref, staged, sem_in)
    load.start()
    load.wait()
    count = out_ref.shape[0]
    copies = []
    for i in range(count):
        copy = pltpu.make_async_copy(
            staged.at[pl.ds(rows_ref[i] * B, B), pl.ds(pl.multiple_of(cols_ref[i] * B, B), B)],
            out_ref.at[i],
            sems_out.at[i],
        )
        copy.start()
        copies.append(copy)
    for copy in copies:
        copy.wait()


def gather_blocks(src, rows, cols):
    count = rows.shape[0]
    grid_spec = pltpu.PrefetchScalarGridSpec(
        num_scalar_prefetch=2,
        grid=(),
        in_specs=[pl.BlockSpec(memory_space=pl.ANY)],
        out_specs=pl.BlockSpec(memory_space=pl.ANY),
        scratch_shapes=[
            pltpu.VMEM(src.shape, src.dtype),
            pltpu.SemaphoreType.DMA(()),
            pltpu.SemaphoreType.DMA((count,)),
        ],
    )
    return pl.pallas_call(
        _copy_blocks,
        out_shape=jax.ShapeDtypeStruct((count, B, B), src.dtype),
        grid_spec=grid_spec,
        cost_estimate=pl.CostEstimate(
            flops=0, bytes_accessed=(src.size + count * B * B) * 4, transcendentals=0
        ),
    )(rows, cols, src)


def select_send(sigma_local, row_blocks, slots):
    own_count = lax.axis_size("own")
    own_here = lax.axis_index("own")
    row_here = lax.axis_index("row")
    rows_here = sigma_local.shape[0] // B
    cols_here = sigma_local.shape[1] // B
    rowlist = row_blocks.reshape(own_count, slots, -1)
    group = own_here * cols_here // rows_here
    want_col = lax.dynamic_index_in_dim(rowlist, group, 2, keepdims=False)
    local_col = want_col - own_here * cols_here
    match = ((local_col >= 0) & (local_col < cols_here)).astype(jnp.int32)
    which = jnp.sum(match * jnp.arange(slots, dtype=jnp.int32)[None, :], axis=1)
    chosen = rowlist[jnp.arange(own_count, dtype=jnp.int32), which]
    chosen_row = jnp.clip(
        lax.dynamic_index_in_dim(chosen, row_here, 1, keepdims=False) - row_here * rows_here,
        0,
        rows_here - 1,
    )
    chosen_col = jnp.clip(
        lax.dynamic_index_in_dim(chosen, group, 1, keepdims=False) - own_here * cols_here,
        0,
        cols_here - 1,
    )
    return gather_blocks(sigma_local, chosen_row, chosen_col)


def _take_blocks(which_ref, src_ref, out_ref, staged, sems_in, sem_out):
    count = staged.shape[0]
    copies = []
    for i in range(count):
        copy = pltpu.make_async_copy(src_ref.at[which_ref[i]], staged.at[i], sems_in.at[i])
        copy.start()
        copies.append(copy)
    for copy in copies:
        copy.wait()
    store = pltpu.make_async_copy(staged, out_ref, sem_out)
    store.start()
    store.wait()


def select_take(received, row_blocks, slots, cols_here):
    mine = lax.axis_index("own") * slots + jnp.arange(slots, dtype=jnp.int32)
    rowlist = row_blocks[mine]
    sender = jnp.clip(rowlist // cols_here, 0, received.shape[0] - 1).reshape(-1)
    count = sender.shape[0]
    grid_spec = pltpu.PrefetchScalarGridSpec(
        num_scalar_prefetch=1,
        grid=(),
        in_specs=[pl.BlockSpec(memory_space=pl.ANY)],
        out_specs=pl.BlockSpec(memory_space=pl.ANY),
        scratch_shapes=[
            pltpu.VMEM((count, B, B), received.dtype),
            pltpu.SemaphoreType.DMA((count,)),
            pltpu.SemaphoreType.DMA(()),
        ],
    )
    taken = pl.pallas_call(
        _take_blocks,
        out_shape=jax.ShapeDtypeStruct((count, B, B), received.dtype),
        grid_spec=grid_spec,
        cost_estimate=pl.CostEstimate(
            flops=0, bytes_accessed=2 * count * B * B * 4, transcendentals=0
        ),
    )(sender, received)
    return taken.reshape(slots, -1, B, B)


def on_device(
    sigma_anc, row_blocks, panel1, diag_inv1, mask1, parent_block2, panel2, diag_inv2, mask2
):
    slots = panel1.shape[0]
    cols_here = sigma_anc.shape[1] // B
    row_count = lax.axis_size("row")
    row_here = lax.axis_index("row")
    keep_own2 = mask2.astype(jnp.float32)
    factor2_own = keep_own2[:, :, None] * product("kij,kjc->kic", panel2, diag_inv2)
    piece = B // row_count
    up_own = lax.dynamic_slice_in_dim(parent_block2, row_here * piece, piece, axis=1)
    up_own = product("kij,kjc->kic", up_own, diag_inv2)
    factor2_child = shifted(factor2_own, "own", -1)
    up_child = shifted(up_own, "own", -1)

    outgoing = select_send(sigma_anc, row_blocks, slots)
    factor2_child, up_child, outgoing = lax.optimization_barrier(
        (factor2_child, up_child, outgoing)
    )
    received = lax.all_to_all(outgoing, "own", split_axis=0, concat_axis=0, tiled=True)

    keep1 = mask1.astype(jnp.float32)
    factor1 = keep1[:, :, None] * product("kij,kjc->kic", panel1, diag_inv1)
    factor2 = keep1[:, :, None] * factor2_child
    both = jnp.concatenate([factor1, factor2], axis=-1)
    boths = row_gather(both)
    up_parent = row_gather(up_child)
    up_parent = up_parent.transpose(1, 0, 2, 3).reshape(slots, B, B)

    blocks1 = select_take(received, row_blocks, slots, cols_here)
    kept = keep1[:, :, None] * product("kmij,mkjc->kic", blocks1, boths)
    sel1_panel = -kept[:, :, :B]
    pre2 = -(product("kij,kjc->kic", sel1_panel, up_parent) + kept[:, :, B:])
    pre2_child = shifted(pre2, "own", 1)
    terms = jnp.concatenate(
        [
            product("kji,kjc->kic", factor1, sel1_panel),
            product("kji,kjc->kic", sel1_panel, factor2),
            product("kji,kjc->kic", factor2, pre2),
        ],
        axis=-1,
    )
    summed = row_scatter(terms)
    pre2_child, summed = lax.optimization_barrier((pre2_child, summed))
    gram1 = product("kji,kjc->kic", diag_inv1, diag_inv1)
    diag_piece = held_rows(gram1) - summed[:, :, :B]
    parent_piece = -(product("kij,kjc->kic", diag_piece, up_parent) + summed[:, :, B : 2 * B])
    sel1_diag = row_rows(diag_piece)
    child = row_rows(
        shifted(jnp.concatenate([parent_piece, summed[:, :, 2 * B :]], axis=-1), "own", 1)
    )
    sel2_parent_child = child[:, :, :B]
    up_own_full = product("kij,kjc->kic", parent_block2, diag_inv2)

    sel2_panel = keep_own2[:, :, None] * pre2_child
    gram2 = product("kji,kjc->kic", diag_inv2, diag_inv2)
    sel2_diag = gram2 - product("kji,kjc->kic", up_own_full, sel2_parent_child) - child[:, :, B:]
    return (sel1_panel, sel1_diag, sel2_parent_child, sel2_panel, sel2_diag)


def solution(mesh):
    in_specs = (
        P("row", "own"),
        P(),
        P("own", "row", None),
        P("own", None, None),
        P("own", "row"),
        P("own", None, None),
        P("own", "row", None),
        P("own", None, None),
        P("own", "row"),
    )
    out_specs = (
        P("own", "row", None),
        P("own", None, None),
        P("own", None, None),
        P("own", "row", None),
        P("own", None, None),
    )
    return jax.shard_map(
        on_device, mesh=mesh, in_specs=in_specs, out_specs=out_specs, check_vma=False
    )
```
